128 devices in a mesh: blk: 8 (over z, x_lo), rep: 16 (over x_hi, y, core).
Axes of the slice: x: 4 (x_hi: 2, x_lo: 2; x = x_hi * 2 + x_lo), y: 4, z: 4, core: 2. Of those that a mesh axis runs over, the one named last changes fastest.
Arguments:
- raw_features: bfloat16 [131072, 512], P(('blk', 'rep')), may hold values from -6 to 6
- move_plan: int32 [8, 16, 16], P('blk'), may hold values from 8 to 64, as said below
- weight: bfloat16 [512, 512], replicated, may hold values from -0.25 to 0.25
- bias_vector: float32 [512], replicated, may hold values from -3 to 3
- tile_rows: int32 [8, 16, 16, 6], P('blk', 'rep'), may hold values from 0 to 31, as said below
- tile_values: bfloat16 [8, 16, 16, 6, 256, 256], P('blk', 'rep'), may hold values from -0.0546875 to 0.0546875
- grad_out: bfloat16 [65536, 512], P(('blk', 'rep')), may hold values from -6 to 6
Outputs:
- projected: bfloat16 [65536, 512], P(('blk', 'rep'))
- activated: bfloat16 [65536, 512], P(('blk', 'rep'))
- feature_grad: bfloat16 [65536, 512], P(('blk', 'rep'))
- weight_grad: float32 [512, 512], replicated
- bias_grad: float32 [512], replicated
The draws below stay inside these ranges and needn't reach their ends.
Inputs may be any that keep to these rules, and one draw needn't show every extreme that they name: For every partition p and destination e the counts move_plan[p, s, e] over sources s sum to 512; the counts of one source over destinations sum to at most 1024, and some source of every partition sends 64 rows to every destination. `tile_rows`: the 6 row tiles listed for one column tile of a device are distinct.
All inputs are finite; a program needn't handle non-finite values.
Results may differ from the reference program's by a relative error of at most 0.018.
Values may be sent and summed in bfloat16 or wider, within the bound.
No kernel may reach another device: no remote copies, remote signals or barrier semaphores. Data moves between devices by JAX's collectives and lax.ppermute only.
A program may use at most 192 MiB of HBM per device.

```python
import math
import jax
import jax.numpy as jnp
from jax import lax

WIDTH = 512
DEV_ROWS = 512
TILE_SIZE = 256
FILL_TILES = 6
ROW_TILES = 32
COL_TILES = 16
PART_ROWS = 8192
RAW_ROWS = 1024
NODE_COUNT = 65536
N_BLK = 8
N_REP = 16


def draw_move_plan(key, part):
    perm_keys = jax.random.split(jax.random.fold_in(key, 1), N_BLK)

    def one_order(one_key):
        return jax.random.permutation(one_key, N_REP)
    rank_order = jax.vmap(one_order)(perm_keys).astype(jnp.int32)
    levels = jnp.array([1, 1, 2, 4], jnp.int32)[rank_order % 4]
    unit_rows = DEV_ROWS // (2 * N_REP)
    half_unit = unit_rows // 2
    shifts = jax.random.randint(jax.random.fold_in(key, 2), (N_BLK, N_REP // 4, N_REP), -half_unit, half_unit + 1, dtype=jnp.int32)
    pair_index = jnp.broadcast_to((rank_order // 4)[:, :, None], (N_BLK, N_REP, N_REP))
    chosen = jnp.take_along_axis(shifts, pair_index, axis=1)
    sign_pattern = jnp.where(rank_order % 4 == 0, 1, jnp.where(rank_order % 4 == 1, -1, 0)).astype(jnp.int32)
    return (unit_rows * levels[:, :, None] + sign_pattern[:, :, None] * chosen).astype(jnp.int32)


def draw_tile_rows(key, part):
    tile_count = N_BLK * N_REP * COL_TILES
    key_list = jax.random.split(jax.random.fold_in(key, 3), tile_count)

    def pick_rows(one_key):
        return jax.random.permutation(one_key, ROW_TILES)[:FILL_TILES]
    chosen_rows = jax.vmap(pick_rows)(key_list).astype(jnp.int32)
    return chosen_rows.reshape(N_BLK, N_REP, COL_TILES, FILL_TILES)


def block_scale(key, dims, cuts, least, high):
    def one(axis_at, blocks):
        steps = jax.random.uniform(jax.random.fold_in(jax.random.fold_in(key, 6), axis_at), (blocks,), jnp.float32, least / len(cuts), high / len(cuts))
        return jnp.repeat(jnp.exp(steps), dims[axis_at] // blocks).reshape((-1,) + (1,) * (len(dims) - axis_at - 1))

    level = one(*cuts[0])
    for cut in cuts[1:]:
        level = level * one(*cut)
    return level


def bell_draw(own_key, shape, width, reach, cuts=(), kind=jnp.bfloat16):
    values = width * jax.random.normal(own_key, shape, jnp.float32)
    if cuts:
        values = values * block_scale(own_key, shape, cuts, -0.22, 0.18)
    return jnp.clip(values, -reach, reach).astype(kind)


def setup_inputs(seed: int = 0) -> dict:
    key_of = jax.random.split(jax.random.key(seed), 8)
    raw_features = bell_draw(key_of[0], (N_BLK * N_REP * RAW_ROWS, WIDTH), 1.0, 6.0, ((0, 128),))
    move_plan = draw_move_plan(jax.random.fold_in(key_of[7], 71), 0)
    weight = bell_draw(key_of[2], (WIDTH, WIDTH), WIDTH ** -0.5, 0.25)
    bias_vector = bell_draw(key_of[3], (WIDTH,), 0.5, 3.0, (), jnp.float32)
    tile_rows = draw_tile_rows(jax.random.fold_in(key_of[7], 71), 0)
    tile_values = bell_draw(key_of[5], (N_BLK, N_REP, COL_TILES, FILL_TILES, TILE_SIZE, TILE_SIZE), (N_BLK * FILL_TILES * TILE_SIZE) ** -0.5, 0.0546875, ((0, 8), (1, 16)))
    grad_out = bell_draw(key_of[6], (NODE_COUNT, WIDTH), 1.0, 6.0, ((0, 128),))
    return {"raw_features": raw_features, "move_plan": move_plan, "weight": weight, "bias_vector": bias_vector, "tile_rows": tile_rows, "tile_values": tile_values, "grad_out": grad_out}


def silu_slope(values):
    sigma = jax.nn.sigmoid(values)
    return sigma * (1.0 + values * (1.0 - sigma))

def rebalance(raw_part, counts):
    positions = jnp.arange(DEV_ROWS, dtype=jnp.int32)
    inclusive = jnp.cumsum(counts, axis=0).astype(jnp.int32)
    exclusive = inclusive - counts
    row_start = (jnp.cumsum(counts, axis=1) - counts).astype(jnp.int32)
    sources = lax.optimization_barrier(jnp.sum((inclusive.T[:, None, :] <= positions[None, :, None]).astype(jnp.int32), axis=2))
    offsets = jnp.take_along_axis(exclusive.T, sources, axis=1)
    first_rows = jnp.take_along_axis(row_start.T, sources, axis=1)
    raw_index = (first_rows + positions[None, :] - offsets).astype(jnp.int32)
    return raw_part[sources, raw_index]

def reference(raw_features, move_plan, weight, bias_vector, tile_rows, tile_values, grad_out):
    raw_blocks = raw_features.reshape(N_BLK, N_REP, RAW_ROWS, WIDTH)
    features = jax.vmap(rebalance)(raw_blocks, move_plan).reshape(NODE_COUNT, WIDTH)
    projected = jnp.dot(features, weight, preferred_element_type=jnp.float32).astype(jnp.bfloat16)
    proj_blocks = projected.reshape(N_BLK, N_REP, DEV_ROWS, WIDTH)

    def device_partial(part_index, rep_index):
        column_indices = lax.dynamic_index_in_dim(proj_blocks, rep_index, 1, keepdims=False)
        column_indices = column_indices.reshape(COL_TILES, TILE_SIZE, WIDTH).astype(jnp.float32)
        stacked_tiles = tile_values[part_index, rep_index].astype(jnp.float32)
        matmul_result = jnp.einsum('rwtx,rxo->rwto', stacked_tiles, column_indices)
        targets = tile_rows[part_index, rep_index].reshape(-1)
        reduced_total = jnp.zeros((ROW_TILES, TILE_SIZE, WIDTH), jnp.float32)
        reduced_total = reduced_total.at[targets].add(matmul_result.reshape(-1, TILE_SIZE, WIDTH))
        return reduced_total.reshape(PART_ROWS, WIDTH).astype(jnp.bfloat16)

    def partition_total(part_index):

        def add_device(rep_index, running):
            return running + device_partial(part_index, rep_index).astype(jnp.float32)
        return lax.fori_loop(0, N_REP, add_device, jnp.zeros((PART_ROWS, WIDTH), jnp.float32))
    totals = lax.map(partition_total, jnp.arange(N_BLK, dtype=jnp.int32))
    preact = totals + bias_vector
    activated = jax.nn.silu(preact).astype(jnp.bfloat16).reshape(NODE_COUNT, WIDTH)
    cotangent = grad_out.reshape(N_BLK, PART_ROWS, WIDTH).astype(jnp.float32)
    pre_grad = (cotangent * silu_slope(preact)).astype(jnp.bfloat16)
    root_count = math.sqrt(NODE_COUNT)
    bias_grad = lax.optimization_barrier(jnp.sum(pre_grad.astype(jnp.float32), axis=(0, 1))) / root_count

    def device_term(part_index, rep_index):
        grad_tiles = pre_grad[part_index].reshape(ROW_TILES, TILE_SIZE, WIDTH)
        selected_rows = grad_tiles[tile_rows[part_index, rep_index]].astype(jnp.float32)
        stacked_tiles = tile_values[part_index, rep_index].astype(jnp.float32)
        column_contribution = jnp.einsum('nzqm,nzqg->nmg', stacked_tiles, selected_rows)
        return column_contribution.reshape(N_BLK, DEV_ROWS, WIDTH)

    def rep_total(rep_index):

        def add_part(part_index, running):
            return running + device_term(part_index, rep_index)
        return lax.fori_loop(0, N_BLK, add_part, jnp.zeros((N_BLK, DEV_ROWS, WIDTH), jnp.float32))
    grads = lax.map(rep_total, jnp.arange(N_REP, dtype=jnp.int32))
    proj_grad = jnp.transpose(grads, (1, 0, 2, 3)).reshape(NODE_COUNT, WIDTH).astype(jnp.bfloat16)
    weight_grad = jnp.dot(features.T, proj_grad, preferred_element_type=jnp.float32) / root_count
    feature_grad = jnp.dot(proj_grad, weight.T, preferred_element_type=jnp.float32).astype(jnp.bfloat16)
    return (projected, activated, feature_grad, weight_grad, bias_grad)
```

```python
import functools
import math

import jax
import jax.numpy as jnp
from jax import lax
from jax.experimental import pallas as pl
from jax.experimental.pallas import tpu as pltpu
from jax.sharding import PartitionSpec as P


def silu_slope(values):
    sigma = jax.nn.sigmoid(values)
    return sigma * (1.0 + values * (1.0 - sigma))


def _forward_kernel(rows_ref, tiles_ref, cols_ref, out_ref, acc_ref):
    step = pl.program_id(0)
    fill = tiles_ref.shape[1]

    @pl.when(step == 0)
    def _():
        acc_ref[...] = jnp.zeros_like(acc_ref)

    inputs = cols_ref[...]
    for j in range(fill):
        target = rows_ref[step, j]
        acc_ref[target] += jnp.dot(tiles_ref[0, j], inputs, preferred_element_type=jnp.float32)

    @pl.when(step == pl.num_programs(0) - 1)
    def _():
        out_ref[...] = acc_ref[...].astype(out_ref.dtype)


def forward_spmm(row_lists, tile_stack, shard_rows, row_tiles, interpret=False):
    col_tiles, fill, tile_size, _ = tile_stack.shape
    width = shard_rows.shape[1]
    grid_spec = pltpu.PrefetchScalarGridSpec(
        num_scalar_prefetch=1,
        grid=(col_tiles,),
        in_specs=[
            pl.BlockSpec((1, fill, tile_size, tile_size), lambda c, rows: (c, 0, 0, 0)),
            pl.BlockSpec((tile_size, width), lambda c, rows: (c, 0)),
        ],
        out_specs=pl.BlockSpec((row_tiles, tile_size, width), lambda c, rows: (0, 0, 0)),
        scratch_shapes=[pltpu.VMEM((row_tiles, tile_size, width), jnp.float32)],
    )
    return pl.pallas_call(
        _forward_kernel,
        grid_spec=grid_spec,
        out_shape=jax.ShapeDtypeStruct((row_tiles, tile_size, width), jnp.bfloat16),
        compiler_params=pltpu.CompilerParams(
            dimension_semantics=("arbitrary",), vmem_limit_bytes=56 * 1024 * 1024
        ),
        interpret=interpret,
    )(row_lists, tile_stack, shard_rows)


def _backward_kernel(rows_ref, tiles_ref, grad_ref, out_ref):
    step = pl.program_id(0)
    fill = tiles_ref.shape[1]
    total = None
    for j in range(fill):
        source = rows_ref[step, j]
        part = lax.dot_general(
            tiles_ref[0, j],
            grad_ref[source],
            (((0,), (0,)), ((), ())),
            preferred_element_type=jnp.float32,
        )
        total = part if total is None else total + part
    out_ref[...] = total.astype(out_ref.dtype)


def backward_spmm(row_lists, tile_stack, grad_tiles, interpret=False):
    col_tiles, fill, tile_size, _ = tile_stack.shape
    row_tiles, _, width = grad_tiles.shape
    grid_spec = pltpu.PrefetchScalarGridSpec(
        num_scalar_prefetch=1,
        grid=(col_tiles,),
        in_specs=[
            pl.BlockSpec((1, fill, tile_size, tile_size), lambda c, rows: (c, 0, 0, 0)),
            pl.BlockSpec((row_tiles, tile_size, width), lambda c, rows: (0, 0, 0)),
        ],
        out_specs=pl.BlockSpec((tile_size, width), lambda c, rows: (c, 0)),
    )
    return pl.pallas_call(
        _backward_kernel,
        grid_spec=grid_spec,
        out_shape=jax.ShapeDtypeStruct((col_tiles * tile_size, width), jnp.bfloat16),
        compiler_params=pltpu.CompilerParams(
            dimension_semantics=("arbitrary",), vmem_limit_bytes=56 * 1024 * 1024
        ),
        interpret=interpret,
    )(row_lists, tile_stack, grad_tiles)


def per_device(raw_features, move_plan, weight, bias_vector, tile_rows, tile_values, grad_out):
    rep_size = lax.axis_size("rep")
    own_index = lax.axis_index("rep")
    dev_rows, feature_width = grad_out.shape
    raw_rows = raw_features.shape[0]
    capacity = 4 * (dev_rows // (2 * rep_size))
    counts = move_plan[0]
    tile_stack = tile_values[0, 0]
    row_lists = tile_rows[0, 0]
    tile_size = tile_stack.shape[2]
    row_tiles = rep_size * dev_rows // tile_size
    root_count = math.sqrt(dev_rows * lax.axis_size("blk") * rep_size)
    sent_counts = lax.dynamic_index_in_dim(counts, own_index, 0, keepdims=False)
    first_rows = jnp.cumsum(sent_counts) - sent_counts
    slot_rows = first_rows[:, None] + jnp.arange(capacity, dtype=jnp.int32)[None, :]
    outgoing = raw_features[jnp.minimum(slot_rows, raw_rows - 1)]
    incoming = lax.all_to_all(outgoing, "rep", split_axis=0, concat_axis=0, tiled=True)
    recv_counts = lax.dynamic_index_in_dim(counts, own_index, 1, keepdims=False)
    inclusive = jnp.cumsum(recv_counts)
    exclusive = inclusive - recv_counts
    positions = jnp.arange(dev_rows, dtype=jnp.int32)
    sources = jnp.sum((inclusive[None, :] <= positions[:, None]).astype(jnp.int32), axis=1)
    selector = sources[:, None] == jnp.arange(rep_size, dtype=jnp.int32)[None, :]
    offsets = jnp.sum(jnp.where(selector, exclusive[None, :], 0), axis=1)
    features = incoming.reshape(rep_size * capacity, feature_width)[
        sources * capacity + positions - offsets
    ]
    projected = jnp.dot(features, weight, preferred_element_type=jnp.float32).astype(jnp.bfloat16)
    shard_rows = lax.all_gather(projected, "blk", axis=0, tiled=True)

    partial_value = forward_spmm(row_lists, tile_stack, shard_rows, row_tiles)
    partial_value = partial_value.reshape(row_tiles * tile_size, feature_width)
    preact = (
        lax.psum_scatter(partial_value, "rep", scatter_dimension=0, tiled=True).astype(jnp.float32)
        + bias_vector
    )
    own_grad = (grad_out.astype(jnp.float32) * silu_slope(preact)).astype(jnp.bfloat16)
    pre_grad = lax.all_gather(own_grad, "rep", axis=0, tiled=True)
    activated = jax.nn.silu(preact).astype(jnp.bfloat16)
    grad_tiles = pre_grad.reshape(row_tiles, tile_size, feature_width)
    column_contribution = backward_spmm(row_lists, tile_stack, grad_tiles)
    proj_grad = lax.psum_scatter(column_contribution, "blk", scatter_dimension=0, tiled=True)
    local_weight = jnp.einsum("nf,ng->fg", features, proj_grad, preferred_element_type=jnp.float32)
    local_bias = jnp.sum(own_grad.astype(jnp.float32), axis=0)
    pad_rows = jnp.zeros((7, feature_width), jnp.float32)
    stacked = jnp.concatenate([local_weight, local_bias[None, :], pad_rows], axis=0)
    stacked_sum = lax.psum(stacked, ("blk", "rep"))
    weight_sum = stacked_sum[:feature_width]
    bias_sum = stacked_sum[feature_width]
    feature_grad = jnp.einsum(
        "ng,fg->nf", proj_grad, weight, preferred_element_type=jnp.float32
    ).astype(jnp.bfloat16)
    return (projected, activated, feature_grad, weight_sum / root_count, bias_sum / root_count)


def solution(mesh):
    return jax.shard_map(
        per_device,
        mesh=mesh,
        in_specs=(
            P(("blk", "rep"), None),
            P("blk", None, None),
            P(),
            P(),
            P("blk", "rep", None, None),
            P("blk", "rep", None, None, None, None),
            P(("blk", "rep"), None),
        ),
        out_specs=(
            P(("blk", "rep"), None),
            P(("blk", "rep"), None),
            P(("blk", "rep"), None),
            P(),
            P(),
        ),
        check_vma=False,
    )
```

```python
import functools
import math

import jax
import jax.numpy as jnp
from jax import lax
from jax.experimental import pallas as pl
from jax.experimental.pallas import tpu as pltpu
from jax.sharding import PartitionSpec as P


def silu_slope(values):
    sigma = jax.nn.sigmoid(values)
    return sigma * (1.0 + values * (1.0 - sigma))


def _forward_kernel(rows_ref, tiles_ref, cols_ref, out_ref, acc_ref):
    step = pl.program_id(0)
    fill = tiles_ref.shape[1]

    @pl.when(step == 0)
    def _():
        acc_ref[...] = jnp.zeros_like(acc_ref)

    inputs = cols_ref[...]
    for j in range(fill):
        target = rows_ref[step, j]
        acc_ref[target] += jnp.dot(tiles_ref[0, j], inputs, preferred_element_type=jnp.float32)

    @pl.when(step == pl.num_programs(0) - 1)
    def _():
        out_ref[...] = acc_ref[...].astype(out_ref.dtype)


def forward_spmm(row_lists, tile_stack, shard_rows, row_tiles, interpret=False):
    col_tiles, fill, tile_size, _ = tile_stack.shape
    width = shard_rows.shape[1]
    grid_spec = pltpu.PrefetchScalarGridSpec(
        num_scalar_prefetch=1,
        grid=(col_tiles,),
        in_specs=[
            pl.BlockSpec((1, fill, tile_size, tile_size), lambda c, rows: (c, 0, 0, 0)),
            pl.BlockSpec((tile_size, width), lambda c, rows: (c, 0)),
        ],
        out_specs=pl.BlockSpec((row_tiles, tile_size, width), lambda c, rows: (0, 0, 0)),
        scratch_shapes=[pltpu.VMEM((row_tiles, tile_size, width), jnp.float32)],
    )
    return pl.pallas_call(
        _forward_kernel,
        grid_spec=grid_spec,
        out_shape=jax.ShapeDtypeStruct((row_tiles, tile_size, width), jnp.bfloat16),
        compiler_params=pltpu.CompilerParams(
            dimension_semantics=("arbitrary",), vmem_limit_bytes=56 * 1024 * 1024
        ),
        interpret=interpret,
    )(row_lists, tile_stack, shard_rows)


def _backward_kernel(rows_ref, tiles_ref, grad_ref, out_ref):
    step = pl.program_id(0)
    fill = tiles_ref.shape[1]
    total = None
    for j in range(fill):
        source = rows_ref[step, j]
        part = lax.dot_general(
            tiles_ref[0, j],
            grad_ref[source],
            (((0,), (0,)), ((), ())),
            preferred_element_type=jnp.float32,
        )
        total = part if total is None else total + part
    out_ref[...] = total.astype(out_ref.dtype)


def backward_spmm(row_lists, tile_stack, grad_tiles, interpret=False):
    col_tiles, fill, tile_size, _ = tile_stack.shape
    row_tiles, _, width = grad_tiles.shape
    grid_spec = pltpu.PrefetchScalarGridSpec(
        num_scalar_prefetch=1,
        grid=(col_tiles,),
        in_specs=[
            pl.BlockSpec((1, fill, tile_size, tile_size), lambda c, rows: (c, 0, 0, 0)),
            pl.BlockSpec((row_tiles, tile_size, width), lambda c, rows: (0, 0, 0)),
        ],
        out_specs=pl.BlockSpec((tile_size, width), lambda c, rows: (c, 0)),
    )
    return pl.pallas_call(
        _backward_kernel,
        grid_spec=grid_spec,
        out_shape=jax.ShapeDtypeStruct((col_tiles * tile_size, width), jnp.bfloat16),
        compiler_params=pltpu.CompilerParams(
            dimension_semantics=("arbitrary",), vmem_limit_bytes=56 * 1024 * 1024
        ),
        interpret=interpret,
    )(row_lists, tile_stack, grad_tiles)


def gather_by_exchange(values, axis, count):
    stacked = jnp.broadcast_to(values[None], (count,) + values.shape)
    return lax.all_to_all(stacked, axis, 0, 0, tiled=True)


def reduce_by_exchange(values, axis, count):
    chunks = values.reshape((count, values.shape[0] // count) + values.shape[1:])
    received = lax.all_to_all(chunks, axis, 0, 0, tiled=True)
    return jnp.sum(received.astype(jnp.float32), axis=0)


def per_device(raw_features, move_plan, weight, bias_vector, tile_rows, tile_values, grad_out):
    rep_size = lax.axis_size("rep")
    own_index = lax.axis_index("rep")
    dev_rows, feature_width = grad_out.shape
    raw_rows = raw_features.shape[0]
    capacity = 4 * (dev_rows // (2 * rep_size))
    counts = move_plan[0]
    tile_stack = tile_values[0, 0]
    row_lists = tile_rows[0, 0]
    tile_size = tile_stack.shape[2]
    row_tiles = rep_size * dev_rows // tile_size
    root_count = math.sqrt(dev_rows * lax.axis_size("blk") * rep_size)
    sent_counts = lax.dynamic_index_in_dim(counts, own_index, 0, keepdims=False)
    first_rows = jnp.cumsum(sent_counts) - sent_counts
    slot_rows = first_rows[:, None] + jnp.arange(capacity, dtype=jnp.int32)[None, :]
    outgoing = raw_features[jnp.minimum(slot_rows, raw_rows - 1)]
    incoming = lax.all_to_all(outgoing, "rep", split_axis=0, concat_axis=0, tiled=True)
    recv_counts = lax.dynamic_index_in_dim(counts, own_index, 1, keepdims=False)
    inclusive = jnp.cumsum(recv_counts)
    exclusive = inclusive - recv_counts
    positions = jnp.arange(dev_rows, dtype=jnp.int32)
    sources = jnp.sum((inclusive[None, :] <= positions[:, None]).astype(jnp.int32), axis=1)
    selector = sources[:, None] == jnp.arange(rep_size, dtype=jnp.int32)[None, :]
    offsets = jnp.sum(jnp.where(selector, exclusive[None, :], 0), axis=1)
    features = incoming.reshape(rep_size * capacity, feature_width)[
        sources * capacity + positions - offsets
    ]
    projected = jnp.dot(features, weight, preferred_element_type=jnp.float32).astype(jnp.bfloat16)
    blk_size = lax.axis_size("blk")
    shard_rows = gather_by_exchange(projected, "blk", blk_size).reshape(-1, feature_width)

    partial_value = forward_spmm(row_lists, tile_stack, shard_rows, row_tiles)
    partial_value = partial_value.reshape(row_tiles * tile_size, feature_width)
    preact = (
        lax.psum_scatter(partial_value, "rep", scatter_dimension=0, tiled=True).astype(jnp.float32)
        + bias_vector
    )
    own_grad = (grad_out.astype(jnp.float32) * silu_slope(preact)).astype(jnp.bfloat16)
    pre_grad = lax.all_gather(own_grad, "rep", axis=0, tiled=True)
    activated = jax.nn.silu(preact).astype(jnp.bfloat16)
    grad_tiles = pre_grad.reshape(row_tiles, tile_size, feature_width)
    column_contribution = backward_spmm(row_lists, tile_stack, grad_tiles)
    proj_grad = reduce_by_exchange(column_contribution, "blk", blk_size).astype(jnp.bfloat16)
    local_weight = jnp.einsum("nf,ng->fg", features, proj_grad, preferred_element_type=jnp.float32)
    local_bias = jnp.sum(own_grad.astype(jnp.float32), axis=0)
    device_count = blk_size * rep_size
    chunk_rows = feature_width // device_count + 1
    pad_rows = jnp.zeros((device_count * chunk_rows - feature_width - 1, feature_width), jnp.float32)
    stacked = jnp.concatenate([local_weight, local_bias[None, :], pad_rows], axis=0)
    reduced = reduce_by_exchange(stacked, ("blk", "rep"), device_count)
    stacked_sum = gather_by_exchange(reduced, ("blk", "rep"), device_count).reshape(
        -1, feature_width
    )
    weight_sum = stacked_sum[:feature_width]
    bias_sum = stacked_sum[feature_width]
    feature_grad = jnp.einsum(
        "ng,fg->nf", proj_grad, weight, preferred_element_type=jnp.float32
    ).astype(jnp.bfloat16)
    return (projected, activated, feature_grad, weight_sum / root_count, bias_sum / root_count)


def solution(mesh):
    return jax.shard_map(
        per_device,
        mesh=mesh,
        in_specs=(
            P(("blk", "rep"), None),
            P("blk", None, None),
            P(),
            P(),
            P("blk", "rep", None, None),
            P("blk", "rep", None, None, None, None),
            P(("blk", "rep"), None),
        ),
        out_specs=(
            P(("blk", "rep"), None),
            P(("blk", "rep"), None),
            P(("blk", "rep"), None),
            P(),
            P(),
        ),
        check_vma=False,
    )
```

```python
import functools
import math

import jax
import jax.numpy as jnp
from jax import lax
from jax.experimental import pallas as pl
from jax.experimental.pallas import tpu as pltpu
from jax.sharding import PartitionSpec as P


def silu_slope(values):
    sigma = jax.nn.sigmoid(values)
    return sigma * (1.0 + values * (1.0 - sigma))


def _forward_kernel(rows_ref, tiles_ref, cols_ref, out_ref, acc_ref):
    step = pl.program_id(0)
    fill = tiles_ref.shape[1]

    @pl.when(step == 0)
    def _():
        acc_ref[...] = jnp.zeros_like(acc_ref)

    inputs = cols_ref[...]
    for j in range(fill):
        target = rows_ref[step, j]
        acc_ref[target] += jnp.dot(tiles_ref[0, j], inputs, preferred_element_type=jnp.float32)

    @pl.when(step == pl.num_programs(0) - 1)
    def _():
        out_ref[...] = acc_ref[...].astype(out_ref.dtype)


def forward_spmm(row_lists, tile_stack, shard_rows, row_tiles, interpret=False):
    col_tiles, fill, tile_size, _ = tile_stack.shape
    width = shard_rows.shape[1]
    grid_spec = pltpu.PrefetchScalarGridSpec(
        num_scalar_prefetch=1,
        grid=(col_tiles,),
        in_specs=[
            pl.BlockSpec((1, fill, tile_size, tile_size), lambda c, rows: (c, 0, 0, 0)),
            pl.BlockSpec((tile_size, width), lambda c, rows: (c, 0)),
        ],
        out_specs=pl.BlockSpec((row_tiles, tile_size, width), lambda c, rows: (0, 0, 0)),
        scratch_shapes=[pltpu.VMEM((row_tiles, tile_size, width), jnp.float32)],
    )
    return pl.pallas_call(
        _forward_kernel,
        grid_spec=grid_spec,
        out_shape=jax.ShapeDtypeStruct((row_tiles, tile_size, width), jnp.bfloat16),
        compiler_params=pltpu.CompilerParams(
            dimension_semantics=("arbitrary",), vmem_limit_bytes=56 * 1024 * 1024
        ),
        interpret=interpret,
    )(row_lists, tile_stack, shard_rows)


def _backward_kernel(rows_ref, tiles_ref, grad_ref, out_ref):
    step = pl.program_id(0)
    fill = tiles_ref.shape[1]
    total = None
    for j in range(fill):
        source = rows_ref[step, j]
        part = lax.dot_general(
            tiles_ref[0, j],
            grad_ref[source],
            (((0,), (0,)), ((), ())),
            preferred_element_type=jnp.float32,
        )
        total = part if total is None else total + part
    out_ref[...] = total.astype(out_ref.dtype)


def backward_spmm(row_lists, tile_stack, grad_tiles, interpret=False):
    col_tiles, fill, tile_size, _ = tile_stack.shape
    row_tiles, _, width = grad_tiles.shape
    grid_spec = pltpu.PrefetchScalarGridSpec(
        num_scalar_prefetch=1,
        grid=(col_tiles,),
        in_specs=[
            pl.BlockSpec((1, fill, tile_size, tile_size), lambda c, rows: (c, 0, 0, 0)),
            pl.BlockSpec((row_tiles, tile_size, width), lambda c, rows: (0, 0, 0)),
        ],
        out_specs=pl.BlockSpec((tile_size, width), lambda c, rows: (c, 0)),
    )
    return pl.pallas_call(
        _backward_kernel,
        grid_spec=grid_spec,
        out_shape=jax.ShapeDtypeStruct((col_tiles * tile_size, width), jnp.bfloat16),
        compiler_params=pltpu.CompilerParams(
            dimension_semantics=("arbitrary",), vmem_limit_bytes=56 * 1024 * 1024
        ),
        interpret=interpret,
    )(row_lists, tile_stack, grad_tiles)


def gather_by_exchange(values, axis, count):
    stacked = jnp.broadcast_to(values[None], (count,) + values.shape)
    return lax.all_to_all(stacked, axis, 0, 0, tiled=True)


def reduce_by_exchange(values, axis, count):
    chunks = values.reshape((count, values.shape[0] // count) + values.shape[1:])
    received = lax.all_to_all(chunks, axis, 0, 0, tiled=True)
    return jnp.sum(received.astype(jnp.float32), axis=0)


def per_device(raw_features, move_plan, weight, bias_vector, tile_rows, tile_values, grad_out):
    rep_size = lax.axis_size("rep")
    own_index = lax.axis_index("rep")
    dev_rows, feature_width = grad_out.shape
    raw_rows = raw_features.shape[0]
    capacity = 4 * (dev_rows // (2 * rep_size))
    counts = move_plan[0]
    tile_stack = tile_values[0, 0]
    row_lists = tile_rows[0, 0]
    tile_size = tile_stack.shape[2]
    row_tiles = rep_size * dev_rows // tile_size
    root_count = math.sqrt(dev_rows * lax.axis_size("blk") * rep_size)
    sent_counts = lax.dynamic_index_in_dim(counts, own_index, 0, keepdims=False)
    first_rows = jnp.cumsum(sent_counts) - sent_counts
    slot_rows = first_rows[:, None] + jnp.arange(capacity, dtype=jnp.int32)[None, :]
    outgoing = raw_features[jnp.minimum(slot_rows, raw_rows - 1)]
    incoming = lax.all_to_all(outgoing, "rep", split_axis=0, concat_axis=0, tiled=True)
    recv_counts = lax.dynamic_index_in_dim(counts, own_index, 1, keepdims=False)
    inclusive = jnp.cumsum(recv_counts)
    exclusive = inclusive - recv_counts
    positions = jnp.arange(dev_rows, dtype=jnp.int32)
    sources = jnp.sum((inclusive[None, :] <= positions[:, None]).astype(jnp.int32), axis=1)
    selector = sources[:, None] == jnp.arange(rep_size, dtype=jnp.int32)[None, :]
    offsets = jnp.sum(jnp.where(selector, exclusive[None, :], 0), axis=1)
    features = incoming.reshape(rep_size * capacity, feature_width)[
        sources * capacity + positions - offsets
    ]
    projected = jnp.dot(features, weight, preferred_element_type=jnp.float32).astype(jnp.bfloat16)
    blk_size = lax.axis_size("blk")
    chunks = 2
    chunk_width = feature_width // chunks
    activated_parts = []
    grad_parts = []
    bias_parts = []
    for chunk in range(chunks):
        columns = slice(chunk * chunk_width, (chunk + 1) * chunk_width)
        shard_rows = gather_by_exchange(projected[:, columns], "blk", blk_size).reshape(
            -1, chunk_width
        )
        partial_value = forward_spmm(row_lists, tile_stack, shard_rows, row_tiles)
        partial_value = partial_value.reshape(row_tiles * tile_size, chunk_width)
        preact = (
            lax.psum_scatter(partial_value, "rep", scatter_dimension=0, tiled=True).astype(
                jnp.float32
            )
            + bias_vector[columns]
        )
        own_grad = (grad_out[:, columns].astype(jnp.float32) * silu_slope(preact)).astype(
            jnp.bfloat16
        )
        pre_grad = lax.all_gather(own_grad, "rep", axis=0, tiled=True)
        activated_parts.append(jax.nn.silu(preact).astype(jnp.bfloat16))
        bias_parts.append(jnp.sum(own_grad.astype(jnp.float32), axis=0))
        grad_tiles = pre_grad.reshape(row_tiles, tile_size, chunk_width)
        column_contribution = backward_spmm(row_lists, tile_stack, grad_tiles)
        grad_parts.append(
            reduce_by_exchange(column_contribution, "blk", blk_size).astype(jnp.bfloat16)
        )
    activated = jnp.concatenate(activated_parts, axis=1)
    proj_grad = jnp.concatenate(grad_parts, axis=1)
    local_bias = jnp.concatenate(bias_parts, axis=0)
    local_weight = jnp.einsum("nf,ng->fg", features, proj_grad, preferred_element_type=jnp.float32)
    device_count = blk_size * rep_size
    chunk_rows = feature_width // device_count + 1
    pad_rows = jnp.zeros((device_count * chunk_rows - feature_width - 1, feature_width), jnp.float32)
    stacked = jnp.concatenate([local_weight, local_bias[None, :], pad_rows], axis=0)
    reduced = reduce_by_exchange(stacked, ("blk", "rep"), device_count)
    stacked_sum = gather_by_exchange(reduced, ("blk", "rep"), device_count).reshape(
        -1, feature_width
    )
    weight_sum = stacked_sum[:feature_width]
    bias_sum = stacked_sum[feature_width]
    feature_grad = jnp.einsum(
        "ng,fg->nf", proj_grad, weight, preferred_element_type=jnp.float32
    ).astype(jnp.bfloat16)
    return (projected, activated, feature_grad, weight_sum / root_count, bias_sum / root_count)


def solution(mesh):
    return jax.shard_map(
        per_device,
        mesh=mesh,
        in_specs=(
            P(("blk", "rep"), None),
            P("blk", None, None),
            P(),
            P(),
            P("blk", "rep", None, None),
            P("blk", "rep", None, None, None, None),
            P(("blk", "rep"), None),
        ),
        out_specs=(
            P(("blk", "rep"), None),
            P(("blk", "rep"), None),
            P(("blk", "rep"), None),
            P(),
            P(),
        ),
        check_vma=False,
    )
```

```python
import functools
import math

import jax
import jax.numpy as jnp
from jax import lax
from jax.experimental import pallas as pl
from jax.experimental.pallas import tpu as pltpu
from jax.sharding import Mesh
from jax.sharding import PartitionSpec as P


def silu_slope(values):
    sigma = jax.nn.sigmoid(values)
    return sigma * (1.0 + values * (1.0 - sigma))


def _forward_kernel(rows_ref, tiles_ref, cols_ref, out_ref, acc_ref):
    step = pl.program_id(0)
    fill = tiles_ref.shape[1]

    @pl.when(step == 0)
    def _():
        acc_ref[...] = jnp.zeros_like(acc_ref)

    inputs = cols_ref[...]
    for j in range(fill):
        target = rows_ref[step, j]
        acc_ref[target] += jnp.dot(tiles_ref[0, j], inputs, preferred_element_type=jnp.float32)

    @pl.when(step == pl.num_programs(0) - 1)
    def _():
        out_ref[...] = acc_ref[...].astype(out_ref.dtype)


def forward_spmm(row_lists, tile_stack, shard_rows, row_tiles, interpret=False):
    col_tiles, fill, tile_size, _ = tile_stack.shape
    width = shard_rows.shape[1]
    grid_spec = pltpu.PrefetchScalarGridSpec(
        num_scalar_prefetch=1,
        grid=(col_tiles,),
        in_specs=[
            pl.BlockSpec((1, fill, tile_size, tile_size), lambda c, rows: (c, 0, 0, 0)),
            pl.BlockSpec((tile_size, width), lambda c, rows: (c, 0)),
        ],
        out_specs=pl.BlockSpec((row_tiles, tile_size, width), lambda c, rows: (0, 0, 0)),
        scratch_shapes=[pltpu.VMEM((row_tiles, tile_size, width), jnp.float32)],
    )
    return pl.pallas_call(
        _forward_kernel,
        grid_spec=grid_spec,
        out_shape=jax.ShapeDtypeStruct((row_tiles, tile_size, width), jnp.bfloat16),
        compiler_params=pltpu.CompilerParams(
            dimension_semantics=("arbitrary",), vmem_limit_bytes=56 * 1024 * 1024
        ),
        interpret=interpret,
    )(row_lists, tile_stack, shard_rows)


def _backward_kernel(rows_ref, tiles_ref, grad_ref, out_ref):
    step = pl.program_id(0)
    fill = tiles_ref.shape[1]
    total = None
    for j in range(fill):
        source = rows_ref[step, j]
        part = lax.dot_general(
            tiles_ref[0, j],
            grad_ref[source],
            (((0,), (0,)), ((), ())),
            preferred_element_type=jnp.float32,
        )
        total = part if total is None else total + part
    out_ref[...] = total.astype(out_ref.dtype)


def backward_spmm(row_lists, tile_stack, grad_tiles, interpret=False):
    col_tiles, fill, tile_size, _ = tile_stack.shape
    row_tiles, _, width = grad_tiles.shape
    grid_spec = pltpu.PrefetchScalarGridSpec(
        num_scalar_prefetch=1,
        grid=(col_tiles,),
        in_specs=[
            pl.BlockSpec((1, fill, tile_size, tile_size), lambda c, rows: (c, 0, 0, 0)),
            pl.BlockSpec((row_tiles, tile_size, width), lambda c, rows: (0, 0, 0)),
        ],
        out_specs=pl.BlockSpec((tile_size, width), lambda c, rows: (c, 0)),
    )
    return pl.pallas_call(
        _backward_kernel,
        grid_spec=grid_spec,
        out_shape=jax.ShapeDtypeStruct((col_tiles * tile_size, width), jnp.bfloat16),
        compiler_params=pltpu.CompilerParams(
            dimension_semantics=("arbitrary",), vmem_limit_bytes=56 * 1024 * 1024
        ),
        interpret=interpret,
    )(row_lists, tile_stack, grad_tiles)


def gather_by_exchange(values, axis, count):
    stacked = jnp.broadcast_to(values[None], (count,) + values.shape)
    return lax.all_to_all(stacked, axis, 0, 0, tiled=True)


def reduce_by_exchange(values, axis, count):
    chunks = values.reshape((count, values.shape[0] // count) + values.shape[1:])
    received = lax.all_to_all(chunks, axis, 0, 0, tiled=True)
    return jnp.sum(received.astype(jnp.float32), axis=0)


def per_device(raw_features, move_plan, weight, bias_vector, tile_rows, tile_values, grad_out):
    core_size = lax.axis_size("core")
    chip_size = lax.axis_size("rh")
    rep_size = chip_size * core_size
    own_index = lax.axis_index("rh") * core_size + lax.axis_index("core")
    dev_rows, feature_width = grad_out.shape
    raw_rows = raw_features.shape[0]
    capacity = 4 * (dev_rows // (2 * rep_size))
    counts = move_plan[0]
    tile_stack = tile_values[0, 0]
    tile_lists = tile_rows[0, 0]
    tile_size = tile_stack.shape[2]
    row_tiles = rep_size * dev_rows // tile_size
    root_count = math.sqrt(dev_rows * lax.axis_size("blk") * rep_size)
    sent_counts = lax.dynamic_index_in_dim(counts, own_index, 0, keepdims=False)
    first_rows = jnp.cumsum(sent_counts) - sent_counts
    slot_rows = first_rows[:, None] + jnp.arange(capacity, dtype=jnp.int32)[None, :]
    outgoing = raw_features[jnp.minimum(slot_rows, raw_rows - 1)]
    incoming = lax.all_to_all(outgoing, ("rh", "core"), split_axis=0, concat_axis=0, tiled=True)
    block_tiles = dev_rows // tile_size
    block_of = tile_lists // block_tiles
    row_lists = (
        (block_of % core_size) * (chip_size * block_tiles)
        + (block_of // core_size) * block_tiles
        + tile_lists % block_tiles
    )
    recv_counts = lax.dynamic_index_in_dim(counts, own_index, 1, keepdims=False)
    inclusive = jnp.cumsum(recv_counts)
    exclusive = inclusive - recv_counts
    positions = jnp.arange(dev_rows, dtype=jnp.int32)
    sources = jnp.sum((inclusive[None, :] <= positions[:, None]).astype(jnp.int32), axis=1)
    selector = sources[:, None] == jnp.arange(rep_size, dtype=jnp.int32)[None, :]
    offsets = jnp.sum(jnp.where(selector, exclusive[None, :], 0), axis=1)
    features = incoming.reshape(rep_size * capacity, feature_width)[
        sources * capacity + positions - offsets
    ]
    projected = jnp.dot(features, weight, preferred_element_type=jnp.float32).astype(jnp.bfloat16)
    blk_size = lax.axis_size("blk")
    shard_rows = gather_by_exchange(projected, "blk", blk_size).reshape(-1, feature_width)

    partial_value = forward_spmm(row_lists, tile_stack, shard_rows, row_tiles)
    by_core = partial_value.reshape(row_tiles * tile_size, feature_width)
    core_sum = reduce_by_exchange(by_core, "core", core_size).astype(jnp.bfloat16)
    preact = reduce_by_exchange(core_sum, "rh", chip_size) + bias_vector
    own_grad = (grad_out.astype(jnp.float32) * silu_slope(preact)).astype(jnp.bfloat16)
    chip_grad = gather_by_exchange(own_grad, "rh", chip_size).reshape(-1, feature_width)
    pre_grad = gather_by_exchange(chip_grad, "core", core_size)
    activated = jax.nn.silu(preact).astype(jnp.bfloat16)
    grad_tiles = pre_grad.reshape(row_tiles, tile_size, feature_width)
    column_contribution = backward_spmm(row_lists, tile_stack, grad_tiles)
    proj_grad = reduce_by_exchange(column_contribution, "blk", blk_size).astype(jnp.bfloat16)
    local_weight = jnp.einsum("nf,ng->fg", features, proj_grad, preferred_element_type=jnp.float32)
    local_bias = jnp.sum(own_grad.astype(jnp.float32), axis=0)
    device_count = blk_size * rep_size
    chunk_rows = feature_width // device_count + 1
    pad_rows = jnp.zeros((device_count * chunk_rows - feature_width - 1, feature_width), jnp.float32)
    stacked = jnp.concatenate([local_weight, local_bias[None, :], pad_rows], axis=0)
    every = ("blk", "rh", "core")
    reduced = reduce_by_exchange(stacked, every, device_count)
    stacked_sum = gather_by_exchange(reduced, every, device_count).reshape(
        -1, feature_width
    )
    weight_sum = stacked_sum[:feature_width]
    bias_sum = stacked_sum[feature_width]
    feature_grad = jnp.einsum(
        "ng,fg->nf", proj_grad, weight, preferred_element_type=jnp.float32
    ).astype(jnp.bfloat16)
    return (projected, activated, feature_grad, weight_sum / root_count, bias_sum / root_count)


def solution(mesh):
    blk_count, rep_count = mesh.devices.shape
    chip_mesh = Mesh(mesh.devices.reshape(blk_count, rep_count // 2, 2), ("blk", "rh", "core"))
    return jax.shard_map(
        per_device,
        mesh=chip_mesh,
        in_specs=(
            P(("blk", "rh", "core"), None),
            P("blk", None, None),
            P(),
            P(),
            P("blk", ("rh", "core"), None, None),
            P("blk", ("rh", "core"), None, None, None, None),
            P(("blk", "rh", "core"), None),
        ),
        out_specs=(
            P(("blk", "rh", "core"), None),
            P(("blk", "rh", "core"), None),
            P(("blk", "rh", "core"), None),
            P(),
            P(),
        ),
        check_vma=False,
    )
```

```python
import functools
import math

import jax
import jax.numpy as jnp
from jax import lax
from jax.experimental import pallas as pl
from jax.experimental.pallas import tpu as pltpu
from jax.sharding import Mesh
from jax.sharding import PartitionSpec as P


def silu_slope(values):
    sigma = jax.nn.sigmoid(values)
    return sigma * (1.0 + values * (1.0 - sigma))


def _forward_kernel(rows_ref, tiles_ref, cols_ref, out_ref, acc_ref):
    step = pl.program_id(0)
    fill = tiles_ref.shape[1]

    @pl.when(step == 0)
    def _():
        acc_ref[...] = jnp.zeros_like(acc_ref)

    inputs = cols_ref[...]
    for j in range(fill):
        target = rows_ref[step, j]
        acc_ref[target] += jnp.dot(tiles_ref[0, j], inputs, preferred_element_type=jnp.float32)

    @pl.when(step == pl.num_programs(0) - 1)
    def _():
        out_ref[...] = acc_ref[...].astype(out_ref.dtype)


def forward_spmm(row_lists, tile_stack, shard_rows, row_tiles, interpret=False):
    col_tiles, fill, tile_size, _ = tile_stack.shape
    width = shard_rows.shape[1]
    grid_spec = pltpu.PrefetchScalarGridSpec(
        num_scalar_prefetch=1,
        grid=(col_tiles,),
        in_specs=[
            pl.BlockSpec((1, fill, tile_size, tile_size), lambda c, rows: (c, 0, 0, 0)),
            pl.BlockSpec((tile_size, width), lambda c, rows: (c, 0)),
        ],
        out_specs=pl.BlockSpec((row_tiles, tile_size, width), lambda c, rows: (0, 0, 0)),
        scratch_shapes=[pltpu.VMEM((row_tiles, tile_size, width), jnp.float32)],
    )
    return pl.pallas_call(
        _forward_kernel,
        grid_spec=grid_spec,
        out_shape=jax.ShapeDtypeStruct((row_tiles, tile_size, width), jnp.bfloat16),
        compiler_params=pltpu.CompilerParams(
            dimension_semantics=("arbitrary",), vmem_limit_bytes=56 * 1024 * 1024
        ),
        interpret=interpret,
    )(row_lists, tile_stack, shard_rows)


def _backward_kernel(rows_ref, tiles_ref, grad_ref, out_ref):
    step = pl.program_id(0)
    fill = tiles_ref.shape[1]
    total = None
    for j in range(fill):
        source = rows_ref[step, j]
        part = lax.dot_general(
            tiles_ref[0, j],
            grad_ref[source],
            (((0,), (0,)), ((), ())),
            preferred_element_type=jnp.float32,
        )
        total = part if total is None else total + part
    out_ref[...] = total.astype(out_ref.dtype)


def backward_spmm(row_lists, tile_stack, grad_tiles, interpret=False):
    col_tiles, fill, tile_size, _ = tile_stack.shape
    row_tiles, _, width = grad_tiles.shape
    grid_spec = pltpu.PrefetchScalarGridSpec(
        num_scalar_prefetch=1,
        grid=(col_tiles,),
        in_specs=[
            pl.BlockSpec((1, fill, tile_size, tile_size), lambda c, rows: (c, 0, 0, 0)),
            pl.BlockSpec((row_tiles, tile_size, width), lambda c, rows: (0, 0, 0)),
        ],
        out_specs=pl.BlockSpec((tile_size, width), lambda c, rows: (c, 0)),
    )
    return pl.pallas_call(
        _backward_kernel,
        grid_spec=grid_spec,
        out_shape=jax.ShapeDtypeStruct((col_tiles * tile_size, width), jnp.bfloat16),
        compiler_params=pltpu.CompilerParams(
            dimension_semantics=("arbitrary",), vmem_limit_bytes=56 * 1024 * 1024
        ),
        interpret=interpret,
    )(row_lists, tile_stack, grad_tiles)


def gather_by_exchange(values, axis, count):
    stacked = jnp.broadcast_to(values[None], (count,) + values.shape)
    return lax.all_to_all(stacked, axis, 0, 0, tiled=True)


def reduce_by_exchange(values, axis, count):
    chunks = values.reshape((count, values.shape[0] // count) + values.shape[1:])
    received = lax.all_to_all(chunks, axis, 0, 0, tiled=True)
    return jnp.sum(received.astype(jnp.float32), axis=0)


def per_device(raw_features, move_plan, weight, bias_vector, tile_rows, tile_values, grad_out):
    core_size = lax.axis_size("core")
    chip_size = lax.axis_size("rh")
    rep_size = chip_size * core_size
    own_index = lax.axis_index("rh") * core_size + lax.axis_index("core")
    dev_rows, feature_width = grad_out.shape
    raw_rows = raw_features.shape[0]
    capacity = 4 * (dev_rows // (2 * rep_size))
    counts = move_plan[0]
    tile_stack = tile_values[0, 0]
    tile_lists = tile_rows[0, 0]
    tile_size = tile_stack.shape[2]
    row_tiles = rep_size * dev_rows // tile_size
    root_count = math.sqrt(dev_rows * lax.axis_size("blk") * rep_size)
    sent_counts = lax.dynamic_index_in_dim(counts, own_index, 0, keepdims=False)
    first_rows = jnp.cumsum(sent_counts) - sent_counts
    slot_rows = first_rows[:, None] + jnp.arange(capacity, dtype=jnp.int32)[None, :]
    outgoing = raw_features[jnp.minimum(slot_rows, raw_rows - 1)]
    incoming = lax.all_to_all(outgoing, ("rh", "core"), split_axis=0, concat_axis=0, tiled=True)
    block_tiles = dev_rows // tile_size
    block_of = tile_lists // block_tiles
    row_lists = (
        (block_of % core_size) * (chip_size * block_tiles)
        + (block_of // core_size) * block_tiles
        + tile_lists % block_tiles
    )
    recv_counts = lax.dynamic_index_in_dim(counts, own_index, 1, keepdims=False)
    inclusive = jnp.cumsum(recv_counts)
    exclusive = inclusive - recv_counts
    positions = jnp.arange(dev_rows, dtype=jnp.int32)
    sources = jnp.sum((inclusive[None, :] <= positions[:, None]).astype(jnp.int32), axis=1)
    selector = sources[:, None] == jnp.arange(rep_size, dtype=jnp.int32)[None, :]
    offsets = jnp.sum(jnp.where(selector, exclusive[None, :], 0), axis=1)
    features = incoming.reshape(rep_size * capacity, feature_width)[
        sources * capacity + positions - offsets
    ]
    projected = jnp.dot(features, weight, preferred_element_type=jnp.float32).astype(jnp.bfloat16)
    blk_size = lax.axis_size("blk")
    chunks = 2
    chunk_width = feature_width // chunks
    activated_parts = []
    grad_parts = []
    bias_parts = []
    for chunk in range(chunks):
        columns = slice(chunk * chunk_width, (chunk + 1) * chunk_width)
        shard_rows = gather_by_exchange(projected[:, columns], "blk", blk_size).reshape(
            -1, chunk_width
        )
        partial_value = forward_spmm(row_lists, tile_stack, shard_rows, row_tiles)
        by_core = partial_value.reshape(row_tiles * tile_size, chunk_width)
        core_sum = reduce_by_exchange(by_core, "core", core_size).astype(jnp.bfloat16)
        preact = reduce_by_exchange(core_sum, "rh", chip_size) + bias_vector[columns]
        own_grad = (grad_out[:, columns].astype(jnp.float32) * silu_slope(preact)).astype(
            jnp.bfloat16
        )
        activated_parts.append(jax.nn.silu(preact).astype(jnp.bfloat16))
        bias_parts.append(jnp.sum(own_grad.astype(jnp.float32), axis=0))
        chip_grad = gather_by_exchange(own_grad, "rh", chip_size).reshape(-1, chunk_width)
        pre_grad = gather_by_exchange(chip_grad, "core", core_size)
        grad_tiles = pre_grad.reshape(row_tiles, tile_size, chunk_width)
        column_contribution = backward_spmm(row_lists, tile_stack, grad_tiles)
        grad_parts.append(
            reduce_by_exchange(column_contribution, "blk", blk_size).astype(jnp.bfloat16)
        )
    activated = jnp.concatenate(activated_parts, axis=1)
    proj_grad = jnp.concatenate(grad_parts, axis=1)
    local_bias = jnp.concatenate(bias_parts, axis=0)
    local_weight = jnp.einsum("nf,ng->fg", features, proj_grad, preferred_element_type=jnp.float32)
    device_count = blk_size * rep_size
    chunk_rows = feature_width // device_count + 1
    pad_rows = jnp.zeros((device_count * chunk_rows - feature_width - 1, feature_width), jnp.float32)
    stacked = jnp.concatenate([local_weight, local_bias[None, :], pad_rows], axis=0)
    every = ("blk", "rh", "core")
    reduced = reduce_by_exchange(stacked, every, device_count)
    stacked_sum = gather_by_exchange(reduced, every, device_count).reshape(
        -1, feature_width
    )
    weight_sum = stacked_sum[:feature_width]
    bias_sum = stacked_sum[feature_width]
    feature_grad = jnp.einsum(
        "ng,fg->nf", proj_grad, weight, preferred_element_type=jnp.float32
    ).astype(jnp.bfloat16)
    return (projected, activated, feature_grad, weight_sum / root_count, bias_sum / root_count)


def solution(mesh):
    blk_count, rep_count = mesh.devices.shape
    chip_mesh = Mesh(mesh.devices.reshape(blk_count, rep_count // 2, 2), ("blk", "rh", "core"))
    return jax.shard_map(
        per_device,
        mesh=chip_mesh,
        in_specs=(
            P(("blk", "rh", "core"), None),
            P("blk", None, None),
            P(),
            P(),
            P("blk", ("rh", "core"), None, None),
            P("blk", ("rh", "core"), None, None, None, None),
            P(("blk", "rh", "core"), None),
        ),
        out_specs=(
            P(("blk", "rh", "core"), None),
            P(("blk", "rh", "core"), None),
            P(("blk", "rh", "core"), None),
            P(),
            P(),
        ),
        check_vma=False,
    )
```

```python
import functools
import math

import jax
import jax.numpy as jnp
from jax import lax
from jax.experimental import pallas as pl
from jax.experimental.pallas import tpu as pltpu
from jax.sharding import Mesh
from jax.sharding import PartitionSpec as P


def silu_slope(values):
    sigma = jax.nn.sigmoid(values)
    return sigma * (1.0 + values * (1.0 - sigma))


def _forward_kernel(rows_ref, tiles_ref, cols_ref, out_ref, acc_ref):
    step = pl.program_id(0)
    fill = tiles_ref.shape[1]

    @pl.when(step == 0)
    def _():
        acc_ref[...] = jnp.zeros_like(acc_ref)

    inputs = cols_ref[...]
    for j in range(fill):
        target = rows_ref[step, j]
        acc_ref[target] += jnp.dot(tiles_ref[0, j], inputs, preferred_element_type=jnp.float32)

    @pl.when(step == pl.num_programs(0) - 1)
    def _():
        out_ref[...] = acc_ref[...].astype(out_ref.dtype)


def forward_spmm(row_lists, tile_stack, shard_rows, row_tiles, interpret=False):
    col_tiles, fill, tile_size, _ = tile_stack.shape
    width = shard_rows.shape[1]
    grid_spec = pltpu.PrefetchScalarGridSpec(
        num_scalar_prefetch=1,
        grid=(col_tiles,),
        in_specs=[
            pl.BlockSpec((1, fill, tile_size, tile_size), lambda c, rows: (c, 0, 0, 0)),
            pl.BlockSpec((tile_size, width), lambda c, rows: (c, 0)),
        ],
        out_specs=pl.BlockSpec((row_tiles, tile_size, width), lambda c, rows: (0, 0, 0)),
        scratch_shapes=[pltpu.VMEM((row_tiles, tile_size, width), jnp.float32)],
    )
    return pl.pallas_call(
        _forward_kernel,
        grid_spec=grid_spec,
        out_shape=jax.ShapeDtypeStruct((row_tiles, tile_size, width), jnp.bfloat16),
        compiler_params=pltpu.CompilerParams(
            dimension_semantics=("arbitrary",), vmem_limit_bytes=56 * 1024 * 1024
        ),
        interpret=interpret,
    )(row_lists, tile_stack, shard_rows)


def _backward_kernel(rows_ref, tiles_ref, grad_ref, out_ref):
    step = pl.program_id(0)
    fill = tiles_ref.shape[1]
    total = None
    for j in range(fill):
        source = rows_ref[step, j]
        part = lax.dot_general(
            tiles_ref[0, j],
            grad_ref[source],
            (((0,), (0,)), ((), ())),
            preferred_element_type=jnp.float32,
        )
        total = part if total is None else total + part
    out_ref[...] = total.astype(out_ref.dtype)


def backward_spmm(row_lists, tile_stack, grad_tiles, interpret=False):
    col_tiles, fill, tile_size, _ = tile_stack.shape
    row_tiles, _, width = grad_tiles.shape
    grid_spec = pltpu.PrefetchScalarGridSpec(
        num_scalar_prefetch=1,
        grid=(col_tiles,),
        in_specs=[
            pl.BlockSpec((1, fill, tile_size, tile_size), lambda c, rows: (c, 0, 0, 0)),
            pl.BlockSpec((row_tiles, tile_size, width), lambda c, rows: (0, 0, 0)),
        ],
        out_specs=pl.BlockSpec((tile_size, width), lambda c, rows: (c, 0)),
    )
    return pl.pallas_call(
        _backward_kernel,
        grid_spec=grid_spec,
        out_shape=jax.ShapeDtypeStruct((col_tiles * tile_size, width), jnp.bfloat16),
        compiler_params=pltpu.CompilerParams(
            dimension_semantics=("arbitrary",), vmem_limit_bytes=56 * 1024 * 1024
        ),
        interpret=interpret,
    )(row_lists, tile_stack, grad_tiles)


def gather_by_exchange(values, axis, count):
    stacked = jnp.broadcast_to(values[None], (count,) + values.shape)
    return lax.all_to_all(stacked, axis, 0, 0, tiled=True)


def reduce_by_exchange(values, axis, count):
    chunks = values.reshape((count, values.shape[0] // count) + values.shape[1:])
    received = lax.all_to_all(chunks, axis, 0, 0, tiled=True)
    return jnp.sum(received.astype(jnp.float32), axis=0)


def per_device(raw_features, move_plan, weight, bias_vector, tile_rows, tile_values, grad_out):
    core_size = lax.axis_size("core")
    chip_size = lax.axis_size("rh")
    rep_size = chip_size * core_size
    own_index = lax.axis_index("rh") * core_size + lax.axis_index("core")
    dev_rows, feature_width = grad_out.shape
    raw_rows = raw_features.shape[0]
    capacity = 4 * (dev_rows // (2 * rep_size))
    counts = move_plan[0]
    tile_stack = tile_values[0, 0]
    tile_lists = tile_rows[0, 0]
    tile_size = tile_stack.shape[2]
    row_tiles = rep_size * dev_rows // tile_size
    root_count = math.sqrt(dev_rows * lax.axis_size("blk") * rep_size)
    sent_counts = lax.dynamic_index_in_dim(counts, own_index, 0, keepdims=False)
    first_rows = jnp.cumsum(sent_counts) - sent_counts
    slot_rows = first_rows[:, None] + jnp.arange(capacity, dtype=jnp.int32)[None, :]
    outgoing = raw_features[jnp.minimum(slot_rows, raw_rows - 1)]
    incoming = lax.all_to_all(outgoing, ("rh", "core"), split_axis=0, concat_axis=0, tiled=True)
    block_tiles = dev_rows // tile_size
    block_of = tile_lists // block_tiles
    row_lists = (
        (block_of % core_size) * (chip_size * block_tiles)
        + (block_of // core_size) * block_tiles
        + tile_lists % block_tiles
    )
    recv_counts = lax.dynamic_index_in_dim(counts, own_index, 1, keepdims=False)
    inclusive = jnp.cumsum(recv_counts)
    exclusive = inclusive - recv_counts
    positions = jnp.arange(dev_rows, dtype=jnp.int32)
    sources = jnp.sum((inclusive[None, :] <= positions[:, None]).astype(jnp.int32), axis=1)
    selector = sources[:, None] == jnp.arange(rep_size, dtype=jnp.int32)[None, :]
    offsets = jnp.sum(jnp.where(selector, exclusive[None, :], 0), axis=1)
    features = incoming.reshape(rep_size * capacity, feature_width)[
        sources * capacity + positions - offsets
    ]
    projected = jnp.dot(features, weight, preferred_element_type=jnp.float32).astype(jnp.bfloat16)
    blk_size = lax.axis_size("blk")
    chunks = 2
    chunk_width = feature_width // chunks
    activated_parts = []
    grad_parts = []
    bias_parts = []
    for chunk in range(chunks):
        columns = slice(chunk * chunk_width, (chunk + 1) * chunk_width)
        shard_rows = gather_by_exchange(projected[:, columns], "blk", blk_size).reshape(
            -1, chunk_width
        )
        partial_value = forward_spmm(row_lists, tile_stack, shard_rows, row_tiles)
        by_core = partial_value.reshape(row_tiles * tile_size, chunk_width)
        core_sum = reduce_by_exchange(by_core, "core", core_size).astype(jnp.bfloat16)
        preact = reduce_by_exchange(core_sum, "rh", chip_size) + bias_vector[columns]
        own_grad = (grad_out[:, columns].astype(jnp.float32) * silu_slope(preact)).astype(
            jnp.bfloat16
        )
        activated_parts.append(jax.nn.silu(preact).astype(jnp.bfloat16))
        bias_parts.append(jnp.sum(own_grad.astype(jnp.float32), axis=0))
        chip_grad = gather_by_exchange(own_grad, "rh", chip_size).reshape(-1, chunk_width)
        pre_grad = gather_by_exchange(chip_grad, "core", core_size)
        grad_tiles = pre_grad.reshape(row_tiles, tile_size, chunk_width)
        column_contribution = backward_spmm(row_lists, tile_stack, grad_tiles)
        grad_parts.append(
            reduce_by_exchange(column_contribution, "blk", blk_size).astype(jnp.bfloat16)
        )
    activated = jnp.concatenate(activated_parts, axis=1)
    proj_grad = jnp.concatenate(grad_parts, axis=1)
    local_bias = jnp.concatenate(bias_parts, axis=0)
    local_weight = jnp.einsum("nf,ng->fg", features, proj_grad, preferred_element_type=jnp.float32)
    device_count = blk_size * rep_size
    chunk_rows = feature_width // device_count + 1
    pad_rows = jnp.zeros((device_count * chunk_rows - feature_width - 1, feature_width), jnp.float32)
    stacked = jnp.concatenate([local_weight, local_bias[None, :], pad_rows], axis=0)
    every = ("blk", "rh", "core")
    reduced = reduce_by_exchange(stacked, every, device_count)
    stacked_sum = (
        gather_by_exchange(reduced.astype(jnp.bfloat16), every, device_count)
        .reshape(-1, feature_width)
        .astype(jnp.float32)
    )
    weight_sum = stacked_sum[:feature_width]
    bias_sum = stacked_sum[feature_width]
    feature_grad = jnp.einsum(
        "ng,fg->nf", proj_grad, weight, preferred_element_type=jnp.float32
    ).astype(jnp.bfloat16)
    return (projected, activated, feature_grad, weight_sum / root_count, bias_sum / root_count)


def solution(mesh):
    blk_count, rep_count = mesh.devices.shape
    chip_mesh = Mesh(mesh.devices.reshape(blk_count, rep_count // 2, 2), ("blk", "rh", "core"))
    return jax.shard_map(
        per_device,
        mesh=chip_mesh,
        in_specs=(
            P(("blk", "rh", "core"), None),
            P("blk", None, None),
            P(),
            P(),
            P("blk", ("rh", "core"), None, None),
            P("blk", ("rh", "core"), None, None, None, None),
            P(("blk", "rh", "core"), None),
        ),
        out_specs=(
            P(("blk", "rh", "core"), None),
            P(("blk", "rh", "core"), None),
            P(("blk", "rh", "core"), None),
            P(),
            P(),
        ),
        check_vma=False,
    )
```

```python
import functools
import math

import jax
import jax.numpy as jnp
from jax import lax
from jax.experimental import pallas as pl
from jax.experimental.pallas import tpu as pltpu
from jax.sharding import Mesh
from jax.sharding import PartitionSpec as P


def silu_slope(values):
    sigma = jax.nn.sigmoid(values)
    return sigma * (1.0 + values * (1.0 - sigma))


def _forward_kernel(rows_ref, tiles_ref, cols_ref, out_ref, acc_ref):
    step = pl.program_id(0)
    fill = tiles_ref.shape[1]

    @pl.when(step == 0)
    def _():
        acc_ref[...] = jnp.zeros_like(acc_ref)

    inputs = cols_ref[...]
    for j in range(fill):
        target = rows_ref[step, j]
        acc_ref[target] += jnp.dot(tiles_ref[0, j], inputs, preferred_element_type=jnp.float32)

    @pl.when(step == pl.num_programs(0) - 1)
    def _():
        out_ref[...] = acc_ref[...].astype(out_ref.dtype)


def forward_spmm(row_lists, tile_stack, shard_rows, row_tiles, interpret=False):
    col_tiles, fill, tile_size, _ = tile_stack.shape
    width = shard_rows.shape[1]
    grid_spec = pltpu.PrefetchScalarGridSpec(
        num_scalar_prefetch=1,
        grid=(col_tiles,),
        in_specs=[
            pl.BlockSpec((1, fill, tile_size, tile_size), lambda c, rows: (c, 0, 0, 0)),
            pl.BlockSpec((tile_size, width), lambda c, rows: (c, 0)),
        ],
        out_specs=pl.BlockSpec((row_tiles, tile_size, width), lambda c, rows: (0, 0, 0)),
        scratch_shapes=[pltpu.VMEM((row_tiles, tile_size, width), jnp.float32)],
    )
    return pl.pallas_call(
        _forward_kernel,
        grid_spec=grid_spec,
        out_shape=jax.ShapeDtypeStruct((row_tiles, tile_size, width), jnp.bfloat16),
        compiler_params=pltpu.CompilerParams(
            dimension_semantics=("arbitrary",), vmem_limit_bytes=56 * 1024 * 1024
        ),
        interpret=interpret,
    )(row_lists, tile_stack, shard_rows)


def _backward_kernel(rows_ref, tiles_ref, grad_ref, out_ref):
    step = pl.program_id(0)
    fill = tiles_ref.shape[1]
    total = None
    for j in range(fill):
        source = rows_ref[step, j]
        part = lax.dot_general(
            tiles_ref[0, j],
            grad_ref[source],
            (((0,), (0,)), ((), ())),
            preferred_element_type=jnp.float32,
        )
        total = part if total is None else total + part
    out_ref[...] = total.astype(out_ref.dtype)


def backward_spmm(row_lists, tile_stack, grad_tiles, interpret=False):
    col_tiles, fill, tile_size, _ = tile_stack.shape
    row_tiles, _, width = grad_tiles.shape
    grid_spec = pltpu.PrefetchScalarGridSpec(
        num_scalar_prefetch=1,
        grid=(col_tiles,),
        in_specs=[
            pl.BlockSpec((1, fill, tile_size, tile_size), lambda c, rows: (c, 0, 0, 0)),
            pl.BlockSpec((row_tiles, tile_size, width), lambda c, rows: (0, 0, 0)),
        ],
        out_specs=pl.BlockSpec((tile_size, width), lambda c, rows: (c, 0)),
    )
    return pl.pallas_call(
        _backward_kernel,
        grid_spec=grid_spec,
        out_shape=jax.ShapeDtypeStruct((col_tiles * tile_size, width), jnp.bfloat16),
        compiler_params=pltpu.CompilerParams(
            dimension_semantics=("arbitrary",), vmem_limit_bytes=56 * 1024 * 1024
        ),
        interpret=interpret,
    )(row_lists, tile_stack, grad_tiles)


def gather_by_exchange(values, axis, count):
    stacked = jnp.broadcast_to(values[None], (count,) + values.shape)
    return lax.all_to_all(stacked, axis, 0, 0, tiled=True)


def reduce_by_exchange(values, axis, count):
    chunks = values.reshape((count, values.shape[0] // count) + values.shape[1:])
    received = lax.all_to_all(chunks, axis, 0, 0, tiled=True)
    return jnp.sum(received.astype(jnp.float32), axis=0)


def per_device(raw_features, move_plan, weight, bias_vector, tile_rows, tile_values, grad_out):
    core_size = lax.axis_size("core")
    chip_size = lax.axis_size("rh")
    rep_size = chip_size * core_size
    own_index = lax.axis_index("rh") * core_size + lax.axis_index("core")
    dev_rows, feature_width = grad_out.shape
    raw_rows = raw_features.shape[0]
    capacity = 4 * (dev_rows // (2 * rep_size))
    counts = move_plan[0]
    tile_stack = tile_values[0, 0]
    tile_lists = tile_rows[0, 0]
    tile_size = tile_stack.shape[2]
    row_tiles = rep_size * dev_rows // tile_size
    root_count = math.sqrt(dev_rows * lax.axis_size("blk") * rep_size)
    sent_counts = lax.dynamic_index_in_dim(counts, own_index, 0, keepdims=False)
    first_rows = jnp.cumsum(sent_counts) - sent_counts
    window_starts = jnp.minimum(first_rows, raw_rows - capacity)
    outgoing = jax.vmap(lambda start: lax.dynamic_slice_in_dim(raw_features, start, capacity))(
        window_starts
    )
    incoming = lax.all_to_all(outgoing, ("rh", "core"), split_axis=0, concat_axis=0, tiled=True)
    block_tiles = dev_rows // tile_size
    block_of = tile_lists // block_tiles
    row_lists = (
        (block_of % core_size) * (chip_size * block_tiles)
        + (block_of // core_size) * block_tiles
        + tile_lists % block_tiles
    )
    recv_counts = lax.dynamic_index_in_dim(counts, own_index, 1, keepdims=False)
    inclusive = jnp.cumsum(recv_counts)
    exclusive = inclusive - recv_counts
    positions = jnp.arange(dev_rows, dtype=jnp.int32)
    sources = jnp.sum((inclusive[None, :] <= positions[:, None]).astype(jnp.int32), axis=1)
    selector = sources[:, None] == jnp.arange(rep_size, dtype=jnp.int32)[None, :]
    plan_starts = jnp.cumsum(counts, axis=1) - counts
    window_shift = plan_starts - jnp.minimum(plan_starts, raw_rows - capacity)
    recv_shift = lax.dynamic_index_in_dim(window_shift, own_index, 1, keepdims=False)
    offsets = jnp.sum(jnp.where(selector, exclusive[None, :] - recv_shift[None, :], 0), axis=1)
    features = incoming.reshape(rep_size * capacity, feature_width)[
        sources * capacity + positions - offsets
    ]
    projected = jnp.dot(features, weight, preferred_element_type=jnp.float32).astype(jnp.bfloat16)
    blk_size = lax.axis_size("blk")
    chunks = 2
    chunk_width = feature_width // chunks
    activated_parts = []
    grad_parts = []
    bias_parts = []
    for chunk in range(chunks):
        columns = slice(chunk * chunk_width, (chunk + 1) * chunk_width)
        shard_rows = gather_by_exchange(projected[:, columns], "blk", blk_size).reshape(
            -1, chunk_width
        )
        partial_value = forward_spmm(row_lists, tile_stack, shard_rows, row_tiles)
        by_core = partial_value.reshape(row_tiles * tile_size, chunk_width)
        core_sum = reduce_by_exchange(by_core, "core", core_size).astype(jnp.bfloat16)
        preact = reduce_by_exchange(core_sum, "rh", chip_size) + bias_vector[columns]
        own_grad = (grad_out[:, columns].astype(jnp.float32) * silu_slope(preact)).astype(
            jnp.bfloat16
        )
        activated_parts.append(jax.nn.silu(preact).astype(jnp.bfloat16))
        bias_parts.append(jnp.sum(own_grad.astype(jnp.float32), axis=0))
        chip_grad = gather_by_exchange(own_grad, "rh", chip_size).reshape(-1, chunk_width)
        pre_grad = gather_by_exchange(chip_grad, "core", core_size)
        grad_tiles = pre_grad.reshape(row_tiles, tile_size, chunk_width)
        column_contribution = backward_spmm(row_lists, tile_stack, grad_tiles)
        grad_parts.append(
            reduce_by_exchange(column_contribution, "blk", blk_size).astype(jnp.bfloat16)
        )
    activated = jnp.concatenate(activated_parts, axis=1)
    proj_grad = jnp.concatenate(grad_parts, axis=1)
    local_bias = jnp.concatenate(bias_parts, axis=0)
    local_weight = jnp.einsum("nf,ng->fg", features, proj_grad, preferred_element_type=jnp.float32)
    device_count = blk_size * rep_size
    chunk_rows = feature_width // device_count + 1
    pad_rows = jnp.zeros((device_count * chunk_rows - feature_width - 1, feature_width), jnp.float32)
    stacked = jnp.concatenate([local_weight, local_bias[None, :], pad_rows], axis=0)
    every = ("blk", "rh", "core")
    reduced = reduce_by_exchange(stacked, every, device_count)
    stacked_sum = (
        gather_by_exchange(reduced.astype(jnp.bfloat16), every, device_count)
        .reshape(-1, feature_width)
        .astype(jnp.float32)
    )
    weight_sum = stacked_sum[:feature_width]
    bias_sum = stacked_sum[feature_width]
    feature_grad = jnp.einsum(
        "ng,fg->nf", proj_grad, weight, preferred_element_type=jnp.float32
    ).astype(jnp.bfloat16)
    return (projected, activated, feature_grad, weight_sum / root_count, bias_sum / root_count)


def solution(mesh):
    blk_count, rep_count = mesh.devices.shape
    chip_mesh = Mesh(mesh.devices.reshape(blk_count, rep_count // 2, 2), ("blk", "rh", "core"))
    return jax.shard_map(
        per_device,
        mesh=chip_mesh,
        in_specs=(
            P(("blk", "rh", "core"), None),
            P("blk", None, None),
            P(),
            P(),
            P("blk", ("rh", "core"), None, None),
            P("blk", ("rh", "core"), None, None, None, None),
            P(("blk", "rh", "core"), None),
        ),
        out_specs=(
            P(("blk", "rh", "core"), None),
            P(("blk", "rh", "core"), None),
            P(("blk", "rh", "core"), None),
            P(),
            P(),
        ),
        check_vma=False,
    )
```

```python
import functools
import math

import jax
import jax.numpy as jnp
from jax import lax
from jax.experimental import pallas as pl
from jax.experimental.pallas import tpu as pltpu
from jax.sharding import Mesh
from jax.sharding import PartitionSpec as P


def silu_slope(values):
    sigma = jax.nn.sigmoid(values)
    return sigma * (1.0 + values * (1.0 - sigma))


def _forward_kernel(rows_ref, first_ref, touched_ref, tiles_ref, cols_ref, out_ref, acc_ref):
    step = pl.program_id(0)
    fill = tiles_ref.shape[1]
    inputs = cols_ref[...]
    for j in range(fill):
        target = rows_ref[step, j]
        product = jnp.dot(tiles_ref[0, j], inputs, preferred_element_type=jnp.float32)

        @pl.when(first_ref[step, j] == 1)
        def _():
            acc_ref[target] = product

        @pl.when(first_ref[step, j] == 0)
        def _():
            acc_ref[target] += product

    @pl.when(step == pl.num_programs(0) - 1)
    def _():
        for tile in range(acc_ref.shape[0]):

            @pl.when(touched_ref[tile] == 1)
            def _():
                out_ref[tile] = acc_ref[tile].astype(out_ref.dtype)

            @pl.when(touched_ref[tile] == 0)
            def _():
                out_ref[tile] = jnp.zeros(out_ref.shape[1:], out_ref.dtype)


def forward_spmm(row_lists, tile_stack, shard_rows, row_tiles, interpret=False):
    col_tiles, fill, tile_size, _ = tile_stack.shape
    width = shard_rows.shape[1]
    flat = row_lists.reshape(-1)
    order = jnp.arange(flat.shape[0], dtype=jnp.int32)
    same = flat[:, None] == flat[None, :]
    earlier = order[None, :] < order[:, None]
    first_flags = (~jnp.any(same & earlier, axis=1)).astype(jnp.int32).reshape(row_lists.shape)
    tiles = jnp.arange(row_tiles, dtype=jnp.int32)
    touched = jnp.any(flat[None, :] == tiles[:, None], axis=1).astype(jnp.int32)
    grid_spec = pltpu.PrefetchScalarGridSpec(
        num_scalar_prefetch=3,
        grid=(col_tiles,),
        in_specs=[
            pl.BlockSpec((1, fill, tile_size, tile_size), lambda c, rows, first, hit: (c, 0, 0, 0)),
            pl.BlockSpec((tile_size, width), lambda c, rows, first, hit: (c, 0)),
        ],
        out_specs=pl.BlockSpec(
            (row_tiles, tile_size, width), lambda c, rows, first, hit: (0, 0, 0)
        ),
        scratch_shapes=[pltpu.VMEM((row_tiles, tile_size, width), jnp.float32)],
    )
    return pl.pallas_call(
        _forward_kernel,
        grid_spec=grid_spec,
        out_shape=jax.ShapeDtypeStruct((row_tiles, tile_size, width), jnp.bfloat16),
        compiler_params=pltpu.CompilerParams(
            dimension_semantics=("arbitrary",), vmem_limit_bytes=56 * 1024 * 1024
        ),
        interpret=interpret,
    )(row_lists, first_flags, touched, tile_stack, shard_rows)


def _backward_kernel(rows_ref, tiles_ref, grad_ref, out_ref):
    step = pl.program_id(0)
    fill = tiles_ref.shape[1]
    total = None
    for j in range(fill):
        source = rows_ref[step, j]
        part = lax.dot_general(
            tiles_ref[0, j],
            grad_ref[source],
            (((0,), (0,)), ((), ())),
            preferred_element_type=jnp.float32,
        )
        total = part if total is None else total + part
    out_ref[...] = total.astype(out_ref.dtype)


def backward_spmm(row_lists, tile_stack, grad_tiles, interpret=False):
    col_tiles, fill, tile_size, _ = tile_stack.shape
    row_tiles, _, width = grad_tiles.shape
    grid_spec = pltpu.PrefetchScalarGridSpec(
        num_scalar_prefetch=1,
        grid=(col_tiles,),
        in_specs=[
            pl.BlockSpec((1, fill, tile_size, tile_size), lambda c, rows: (c, 0, 0, 0)),
            pl.BlockSpec((row_tiles, tile_size, width), lambda c, rows: (0, 0, 0)),
        ],
        out_specs=pl.BlockSpec((tile_size, width), lambda c, rows: (c, 0)),
    )
    return pl.pallas_call(
        _backward_kernel,
        grid_spec=grid_spec,
        out_shape=jax.ShapeDtypeStruct((col_tiles * tile_size, width), jnp.bfloat16),
        compiler_params=pltpu.CompilerParams(
            dimension_semantics=("arbitrary",), vmem_limit_bytes=56 * 1024 * 1024
        ),
        interpret=interpret,
    )(row_lists, tile_stack, grad_tiles)


def gather_by_exchange(values, axis, count):
    stacked = jnp.broadcast_to(values[None], (count,) + values.shape)
    return lax.all_to_all(stacked, axis, 0, 0, tiled=True)


def reduce_by_exchange(values, axis, count):
    chunks = values.reshape((count, values.shape[0] // count) + values.shape[1:])
    received = lax.all_to_all(chunks, axis, 0, 0, tiled=True)
    return jnp.sum(received.astype(jnp.float32), axis=0)


def per_device(raw_features, move_plan, weight, bias_vector, tile_rows, tile_values, grad_out):
    core_size = lax.axis_size("core")
    chip_size = lax.axis_size("rh")
    rep_size = chip_size * core_size
    own_index = lax.axis_index("rh") * core_size + lax.axis_index("core")
    dev_rows, feature_width = grad_out.shape
    raw_rows = raw_features.shape[0]
    capacity = 4 * (dev_rows // (2 * rep_size))
    counts = move_plan[0]
    tile_stack = tile_values[0, 0]
    tile_lists = tile_rows[0, 0]
    tile_size = tile_stack.shape[2]
    row_tiles = rep_size * dev_rows // tile_size
    root_count = math.sqrt(dev_rows * lax.axis_size("blk") * rep_size)
    sent_counts = lax.dynamic_index_in_dim(counts, own_index, 0, keepdims=False)
    first_rows = jnp.cumsum(sent_counts) - sent_counts
    slot_rows = first_rows[:, None] + jnp.arange(capacity, dtype=jnp.int32)[None, :]
    outgoing = raw_features[jnp.minimum(slot_rows, raw_rows - 1)]
    incoming = lax.all_to_all(outgoing, ("rh", "core"), split_axis=0, concat_axis=0, tiled=True)
    block_tiles = dev_rows // tile_size
    block_of = tile_lists // block_tiles
    row_lists = (
        (block_of % core_size) * (chip_size * block_tiles)
        + (block_of // core_size) * block_tiles
        + tile_lists % block_tiles
    )
    recv_counts = lax.dynamic_index_in_dim(counts, own_index, 1, keepdims=False)
    inclusive = jnp.cumsum(recv_counts)
    exclusive = inclusive - recv_counts
    positions = jnp.arange(dev_rows, dtype=jnp.int32)
    sources = jnp.sum((inclusive[None, :] <= positions[:, None]).astype(jnp.int32), axis=1)
    selector = sources[:, None] == jnp.arange(rep_size, dtype=jnp.int32)[None, :]
    offsets = jnp.sum(jnp.where(selector, exclusive[None, :], 0), axis=1)
    features = incoming.reshape(rep_size * capacity, feature_width)[
        sources * capacity + positions - offsets
    ]
    projected = jnp.dot(features, weight, preferred_element_type=jnp.float32).astype(jnp.bfloat16)
    blk_size = lax.axis_size("blk")
    chunks = 2
    chunk_width = feature_width // chunks
    activated_parts = []
    grad_parts = []
    bias_parts = []
    for chunk in range(chunks):
        columns = slice(chunk * chunk_width, (chunk + 1) * chunk_width)
        shard_rows = gather_by_exchange(projected[:, columns], "blk", blk_size).reshape(
            -1, chunk_width
        )
        partial_value = forward_spmm(row_lists, tile_stack, shard_rows, row_tiles)
        by_core = partial_value.reshape(row_tiles * tile_size, chunk_width)
        core_sum = reduce_by_exchange(by_core, "core", core_size).astype(jnp.bfloat16)
        preact = reduce_by_exchange(core_sum, "rh", chip_size) + bias_vector[columns]
        own_grad = (grad_out[:, columns].astype(jnp.float32) * silu_slope(preact)).astype(
            jnp.bfloat16
        )
        activated_parts.append(jax.nn.silu(preact).astype(jnp.bfloat16))
        bias_parts.append(jnp.sum(own_grad.astype(jnp.float32), axis=0))
        chip_grad = gather_by_exchange(own_grad, "rh", chip_size).reshape(-1, chunk_width)
        pre_grad = gather_by_exchange(chip_grad, "core", core_size)
        grad_tiles = pre_grad.reshape(row_tiles, tile_size, chunk_width)
        column_contribution = backward_spmm(row_lists, tile_stack, grad_tiles)
        grad_parts.append(
            reduce_by_exchange(column_contribution, "blk", blk_size).astype(jnp.bfloat16)
        )
    activated = jnp.concatenate(activated_parts, axis=1)
    proj_grad = jnp.concatenate(grad_parts, axis=1)
    local_bias = jnp.concatenate(bias_parts, axis=0)
    local_weight = jnp.einsum("nf,ng->fg", features, proj_grad, preferred_element_type=jnp.float32)
    device_count = blk_size * rep_size
    chunk_rows = feature_width // device_count + 1
    pad_rows = jnp.zeros((device_count * chunk_rows - feature_width - 1, feature_width), jnp.float32)
    stacked = jnp.concatenate([local_weight, local_bias[None, :], pad_rows], axis=0)
    every = ("blk", "rh", "core")
    reduced = reduce_by_exchange(stacked, every, device_count)
    stacked_sum = (
        gather_by_exchange(reduced.astype(jnp.bfloat16), every, device_count)
        .reshape(-1, feature_width)
        .astype(jnp.float32)
    )
    weight_sum = stacked_sum[:feature_width]
    bias_sum = stacked_sum[feature_width]
    feature_grad = jnp.einsum(
        "ng,fg->nf", proj_grad, weight, preferred_element_type=jnp.float32
    ).astype(jnp.bfloat16)
    return (projected, activated, feature_grad, weight_sum / root_count, bias_sum / root_count)


def solution(mesh):
    blk_count, rep_count = mesh.devices.shape
    chip_mesh = Mesh(mesh.devices.reshape(blk_count, rep_count // 2, 2), ("blk", "rh", "core"))
    return jax.shard_map(
        per_device,
        mesh=chip_mesh,
        in_specs=(
            P(("blk", "rh", "core"), None),
            P("blk", None, None),
            P(),
            P(),
            P("blk", ("rh", "core"), None, None),
            P("blk", ("rh", "core"), None, None, None, None),
            P(("blk", "rh", "core"), None),
        ),
        out_specs=(
            P(("blk", "rh", "core"), None),
            P(("blk", "rh", "core"), None),
            P(("blk", "rh", "core"), None),
            P(),
            P(),
        ),
        check_vma=False,
    )
```

```python
import functools
import math

import jax
import jax.numpy as jnp
from jax import lax
from jax.experimental import pallas as pl
from jax.experimental.pallas import tpu as pltpu
from jax.sharding import Mesh
from jax.sharding import PartitionSpec as P


def silu_slope(values):
    sigma = jax.nn.sigmoid(values)
    return sigma * (1.0 + values * (1.0 - sigma))


def _forward_kernel(rows_ref, first_ref, touched_ref, tiles_ref, cols_ref, out_ref, acc_ref):
    step = pl.program_id(0)
    fill = tiles_ref.shape[1]
    inputs = cols_ref[...]
    for j in range(fill):
        target = rows_ref[step, j]
        product = jnp.dot(tiles_ref[0, j], inputs, preferred_element_type=jnp.float32)
        acc_ref[target] = jnp.where(first_ref[step, j] == 1, product, acc_ref[target] + product)

    @pl.when(step == pl.num_programs(0) - 1)
    def _():
        for tile in range(acc_ref.shape[0]):
            out_ref[tile] = jnp.where(touched_ref[tile] == 1, acc_ref[tile], 0.0).astype(
                out_ref.dtype
            )


def forward_spmm(row_lists, tile_stack, shard_rows, row_tiles, interpret=False):
    col_tiles, fill, tile_size, _ = tile_stack.shape
    width = shard_rows.shape[1]
    flat = row_lists.reshape(-1)
    order = jnp.arange(flat.shape[0], dtype=jnp.int32)
    same = flat[:, None] == flat[None, :]
    earlier = order[None, :] < order[:, None]
    first_flags = (~jnp.any(same & earlier, axis=1)).astype(jnp.int32).reshape(row_lists.shape)
    tiles = jnp.arange(row_tiles, dtype=jnp.int32)
    touched = jnp.any(flat[None, :] == tiles[:, None], axis=1).astype(jnp.int32)
    grid_spec = pltpu.PrefetchScalarGridSpec(
        num_scalar_prefetch=3,
        grid=(col_tiles,),
        in_specs=[
            pl.BlockSpec((1, fill, tile_size, tile_size), lambda c, rows, first, hit: (c, 0, 0, 0)),
            pl.BlockSpec((tile_size, width), lambda c, rows, first, hit: (c, 0)),
        ],
        out_specs=pl.BlockSpec(
            (row_tiles, tile_size, width), lambda c, rows, first, hit: (0, 0, 0)
        ),
        scratch_shapes=[pltpu.VMEM((row_tiles, tile_size, width), jnp.float32)],
    )
    return pl.pallas_call(
        _forward_kernel,
        grid_spec=grid_spec,
        out_shape=jax.ShapeDtypeStruct((row_tiles, tile_size, width), jnp.bfloat16),
        compiler_params=pltpu.CompilerParams(
            dimension_semantics=("arbitrary",), vmem_limit_bytes=56 * 1024 * 1024
        ),
        interpret=interpret,
    )(row_lists, first_flags, touched, tile_stack, shard_rows)


def _backward_kernel(rows_ref, tiles_ref, grad_ref, out_ref):
    step = pl.program_id(0)
    fill = tiles_ref.shape[1]
    total = None
    for j in range(fill):
        source = rows_ref[step, j]
        part = lax.dot_general(
            tiles_ref[0, j],
            grad_ref[source],
            (((0,), (0,)), ((), ())),
            preferred_element_type=jnp.float32,
        )
        total = part if total is None else total + part
    out_ref[...] = total.astype(out_ref.dtype)


def backward_spmm(row_lists, tile_stack, grad_tiles, interpret=False):
    col_tiles, fill, tile_size, _ = tile_stack.shape
    row_tiles, _, width = grad_tiles.shape
    grid_spec = pltpu.PrefetchScalarGridSpec(
        num_scalar_prefetch=1,
        grid=(col_tiles,),
        in_specs=[
            pl.BlockSpec((1, fill, tile_size, tile_size), lambda c, rows: (c, 0, 0, 0)),
            pl.BlockSpec((row_tiles, tile_size, width), lambda c, rows: (0, 0, 0)),
        ],
        out_specs=pl.BlockSpec((tile_size, width), lambda c, rows: (c, 0)),
    )
    return pl.pallas_call(
        _backward_kernel,
        grid_spec=grid_spec,
        out_shape=jax.ShapeDtypeStruct((col_tiles * tile_size, width), jnp.bfloat16),
        compiler_params=pltpu.CompilerParams(
            dimension_semantics=("arbitrary",), vmem_limit_bytes=56 * 1024 * 1024
        ),
        interpret=interpret,
    )(row_lists, tile_stack, grad_tiles)


def gather_by_exchange(values, axis, count):
    stacked = jnp.broadcast_to(values[None], (count,) + values.shape)
    return lax.all_to_all(stacked, axis, 0, 0, tiled=True)


def reduce_by_exchange(values, axis, count):
    chunks = values.reshape((count, values.shape[0] // count) + values.shape[1:])
    received = lax.all_to_all(chunks, axis, 0, 0, tiled=True)
    return jnp.sum(received.astype(jnp.float32), axis=0)


def per_device(raw_features, move_plan, weight, bias_vector, tile_rows, tile_values, grad_out):
    core_size = lax.axis_size("core")
    chip_size = lax.axis_size("rh")
    rep_size = chip_size * core_size
    own_index = lax.axis_index("rh") * core_size + lax.axis_index("core")
    dev_rows, feature_width = grad_out.shape
    raw_rows = raw_features.shape[0]
    capacity = 4 * (dev_rows // (2 * rep_size))
    counts = move_plan[0]
    tile_stack = tile_values[0, 0]
    tile_lists = tile_rows[0, 0]
    tile_size = tile_stack.shape[2]
    row_tiles = rep_size * dev_rows // tile_size
    root_count = math.sqrt(dev_rows * lax.axis_size("blk") * rep_size)
    sent_counts = lax.dynamic_index_in_dim(counts, own_index, 0, keepdims=False)
    first_rows = jnp.cumsum(sent_counts) - sent_counts
    slot_rows = first_rows[:, None] + jnp.arange(capacity, dtype=jnp.int32)[None, :]
    outgoing = raw_features[jnp.minimum(slot_rows, raw_rows - 1)]
    incoming = lax.all_to_all(outgoing, ("rh", "core"), split_axis=0, concat_axis=0, tiled=True)
    block_tiles = dev_rows // tile_size
    block_of = tile_lists // block_tiles
    row_lists = (
        (block_of % core_size) * (chip_size * block_tiles)
        + (block_of // core_size) * block_tiles
        + tile_lists % block_tiles
    )
    recv_counts = lax.dynamic_index_in_dim(counts, own_index, 1, keepdims=False)
    inclusive = jnp.cumsum(recv_counts)
    exclusive = inclusive - recv_counts
    positions = jnp.arange(dev_rows, dtype=jnp.int32)
    sources = jnp.sum((inclusive[None, :] <= positions[:, None]).astype(jnp.int32), axis=1)
    selector = sources[:, None] == jnp.arange(rep_size, dtype=jnp.int32)[None, :]
    offsets = jnp.sum(jnp.where(selector, exclusive[None, :], 0), axis=1)
    features = incoming.reshape(rep_size * capacity, feature_width)[
        sources * capacity + positions - offsets
    ]
    projected = jnp.dot(features, weight, preferred_element_type=jnp.float32).astype(jnp.bfloat16)
    blk_size = lax.axis_size("blk")
    chunks = 2
    chunk_width = feature_width // chunks
    activated_parts = []
    grad_parts = []
    bias_parts = []
    for chunk in range(chunks):
        columns = slice(chunk * chunk_width, (chunk + 1) * chunk_width)
        shard_rows = gather_by_exchange(projected[:, columns], "blk", blk_size).reshape(
            -1, chunk_width
        )
        partial_value = forward_spmm(row_lists, tile_stack, shard_rows, row_tiles)
        by_core = partial_value.reshape(row_tiles * tile_size, chunk_width)
        core_sum = reduce_by_exchange(by_core, "core", core_size).astype(jnp.bfloat16)
        preact = reduce_by_exchange(core_sum, "rh", chip_size) + bias_vector[columns]
        own_grad = (grad_out[:, columns].astype(jnp.float32) * silu_slope(preact)).astype(
            jnp.bfloat16
        )
        activated_parts.append(jax.nn.silu(preact).astype(jnp.bfloat16))
        bias_parts.append(jnp.sum(own_grad.astype(jnp.float32), axis=0))
        chip_grad = gather_by_exchange(own_grad, "rh", chip_size).reshape(-1, chunk_width)
        pre_grad = gather_by_exchange(chip_grad, "core", core_size)
        grad_tiles = pre_grad.reshape(row_tiles, tile_size, chunk_width)
        column_contribution = backward_spmm(row_lists, tile_stack, grad_tiles)
        grad_parts.append(
            reduce_by_exchange(column_contribution, "blk", blk_size).astype(jnp.bfloat16)
        )
    activated = jnp.concatenate(activated_parts, axis=1)
    proj_grad = jnp.concatenate(grad_parts, axis=1)
    local_bias = jnp.concatenate(bias_parts, axis=0)
    local_weight = jnp.einsum("nf,ng->fg", features, proj_grad, preferred_element_type=jnp.float32)
    device_count = blk_size * rep_size
    chunk_rows = feature_width // device_count + 1
    pad_rows = jnp.zeros((device_count * chunk_rows - feature_width - 1, feature_width), jnp.float32)
    stacked = jnp.concatenate([local_weight, local_bias[None, :], pad_rows], axis=0)
    every = ("blk", "rh", "core")
    reduced = reduce_by_exchange(stacked, every, device_count)
    stacked_sum = (
        gather_by_exchange(reduced.astype(jnp.bfloat16), every, device_count)
        .reshape(-1, feature_width)
        .astype(jnp.float32)
    )
    weight_sum = stacked_sum[:feature_width]
    bias_sum = stacked_sum[feature_width]
    feature_grad = jnp.einsum(
        "ng,fg->nf", proj_grad, weight, preferred_element_type=jnp.float32
    ).astype(jnp.bfloat16)
    return (projected, activated, feature_grad, weight_sum / root_count, bias_sum / root_count)


def solution(mesh):
    blk_count, rep_count = mesh.devices.shape
    chip_mesh = Mesh(mesh.devices.reshape(blk_count, rep_count // 2, 2), ("blk", "rh", "core"))
    return jax.shard_map(
        per_device,
        mesh=chip_mesh,
        in_specs=(
            P(("blk", "rh", "core"), None),
            P("blk", None, None),
            P(),
            P(),
            P("blk", ("rh", "core"), None, None),
            P("blk", ("rh", "core"), None, None, None, None),
            P(("blk", "rh", "core"), None),
        ),
        out_specs=(
            P(("blk", "rh", "core"), None),
            P(("blk", "rh", "core"), None),
            P(("blk", "rh", "core"), None),
            P(),
            P(),
        ),
        check_vma=False,
    )
```

```python
import functools
import math

import jax
import jax.numpy as jnp
from jax import lax
from jax.experimental import pallas as pl
from jax.experimental.pallas import tpu as pltpu
from jax.sharding import Mesh
from jax.sharding import PartitionSpec as P


def silu_slope(values):
    sigma = jax.nn.sigmoid(values)
    return sigma * (1.0 + values * (1.0 - sigma))


def _forward_kernel(rows_ref, first_ref, touched_ref, tiles_ref, cols_ref, out_ref, acc_ref):
    step = pl.program_id(0)
    fill = tiles_ref.shape[1]
    inputs = cols_ref[...]
    for j in range(fill):
        target = rows_ref[step, j]
        product = jnp.dot(tiles_ref[0, j], inputs, preferred_element_type=jnp.float32)
        acc_ref[target] = jnp.where(first_ref[step, j] == 1, product, acc_ref[target] + product)

    @pl.when(step == pl.num_programs(0) - 1)
    def _():
        for tile in range(acc_ref.shape[0]):
            out_ref[tile] = jnp.where(touched_ref[tile] == 1, acc_ref[tile], 0.0).astype(
                out_ref.dtype
            )


def forward_spmm(row_lists, tile_stack, shard_rows, row_tiles, interpret=False):
    col_tiles, fill, tile_size, _ = tile_stack.shape
    width = shard_rows.shape[1]
    flat = row_lists.reshape(-1)
    order = jnp.arange(flat.shape[0], dtype=jnp.int32)
    same = flat[:, None] == flat[None, :]
    earlier = order[None, :] < order[:, None]
    first_flags = (~jnp.any(same & earlier, axis=1)).astype(jnp.int32).reshape(row_lists.shape)
    tiles = jnp.arange(row_tiles, dtype=jnp.int32)
    touched = jnp.any(flat[None, :] == tiles[:, None], axis=1).astype(jnp.int32)
    grid_spec = pltpu.PrefetchScalarGridSpec(
        num_scalar_prefetch=3,
        grid=(col_tiles,),
        in_specs=[
            pl.BlockSpec((1, fill, tile_size, tile_size), lambda c, rows, first, hit: (c, 0, 0, 0)),
            pl.BlockSpec((tile_size, width), lambda c, rows, first, hit: (c, 0)),
        ],
        out_specs=pl.BlockSpec(
            (row_tiles, tile_size, width), lambda c, rows, first, hit: (0, 0, 0)
        ),
        scratch_shapes=[pltpu.VMEM((row_tiles, tile_size, width), jnp.float32)],
    )
    return pl.pallas_call(
        _forward_kernel,
        grid_spec=grid_spec,
        out_shape=jax.ShapeDtypeStruct((row_tiles, tile_size, width), jnp.bfloat16),
        compiler_params=pltpu.CompilerParams(
            dimension_semantics=("arbitrary",), vmem_limit_bytes=56 * 1024 * 1024
        ),
        interpret=interpret,
    )(row_lists, first_flags, touched, tile_stack, shard_rows)


def _backward_kernel(rows_ref, tiles_ref, grad_ref, out_ref):
    step = pl.program_id(0)
    fill = tiles_ref.shape[1]
    total = None
    for j in range(fill):
        source = rows_ref[step, j]
        part = lax.dot_general(
            tiles_ref[0, j],
            grad_ref[source],
            (((0,), (0,)), ((), ())),
            preferred_element_type=jnp.float32,
        )
        total = part if total is None else total + part
    out_ref[...] = total.astype(out_ref.dtype)


def backward_spmm(row_lists, tile_stack, grad_tiles, interpret=False):
    col_tiles, fill, tile_size, _ = tile_stack.shape
    row_tiles, _, width = grad_tiles.shape
    grid_spec = pltpu.PrefetchScalarGridSpec(
        num_scalar_prefetch=1,
        grid=(col_tiles,),
        in_specs=[
            pl.BlockSpec((1, fill, tile_size, tile_size), lambda c, rows: (c, 0, 0, 0)),
            pl.BlockSpec((row_tiles, tile_size, width), lambda c, rows: (0, 0, 0)),
        ],
        out_specs=pl.BlockSpec((tile_size, width), lambda c, rows: (c, 0)),
    )
    return pl.pallas_call(
        _backward_kernel,
        grid_spec=grid_spec,
        out_shape=jax.ShapeDtypeStruct((col_tiles * tile_size, width), jnp.bfloat16),
        compiler_params=pltpu.CompilerParams(
            dimension_semantics=("arbitrary",), vmem_limit_bytes=56 * 1024 * 1024
        ),
        interpret=interpret,
    )(row_lists, tile_stack, grad_tiles)


def gather_by_exchange(values, axis, count):
    stacked = jnp.broadcast_to(values[None], (count,) + values.shape)
    return lax.all_to_all(stacked, axis, 0, 0, tiled=True)


def reduce_by_exchange(values, axis, count):
    chunks = values.reshape((count, values.shape[0] // count) + values.shape[1:])
    received = lax.all_to_all(chunks, axis, 0, 0, tiled=True)
    return jnp.sum(received.astype(jnp.float32), axis=0)


def per_device(raw_features, move_plan, weight, bias_vector, tile_rows, tile_values, grad_out):
    core_size = lax.axis_size("core")
    chip_size = lax.axis_size("rh")
    rep_size = chip_size * core_size
    own_index = lax.axis_index("rh") * core_size + lax.axis_index("core")
    dev_rows, feature_width = grad_out.shape
    raw_rows = raw_features.shape[0]
    capacity = 4 * (dev_rows // (2 * rep_size))
    counts = move_plan[0]
    tile_stack = tile_values[0, 0]
    tile_lists = tile_rows[0, 0]
    tile_size = tile_stack.shape[2]
    row_tiles = rep_size * dev_rows // tile_size
    root_count = math.sqrt(dev_rows * lax.axis_size("blk") * rep_size)
    sent_counts = lax.dynamic_index_in_dim(counts, own_index, 0, keepdims=False)
    first_rows = jnp.cumsum(sent_counts) - sent_counts
    slot_rows = first_rows[:, None] + jnp.arange(capacity, dtype=jnp.int32)[None, :]
    outgoing = raw_features[jnp.minimum(slot_rows, raw_rows - 1)]
    incoming = lax.all_to_all(outgoing, ("rh", "core"), split_axis=0, concat_axis=0, tiled=True)
    block_tiles = dev_rows // tile_size
    block_of = tile_lists // block_tiles
    row_lists = (
        (block_of % core_size) * (chip_size * block_tiles)
        + (block_of // core_size) * block_tiles
        + tile_lists % block_tiles
    )
    recv_counts = lax.dynamic_index_in_dim(counts, own_index, 1, keepdims=False)
    inclusive = jnp.cumsum(recv_counts)
    exclusive = inclusive - recv_counts
    positions = jnp.arange(dev_rows, dtype=jnp.int32)
    sources = jnp.sum((inclusive[None, :] <= positions[:, None]).astype(jnp.int32), axis=1)
    selector = sources[:, None] == jnp.arange(rep_size, dtype=jnp.int32)[None, :]
    offsets = jnp.sum(jnp.where(selector, exclusive[None, :], 0), axis=1)
    features = incoming.reshape(rep_size * capacity, feature_width)[
        sources * capacity + positions - offsets
    ]
    projected = jnp.dot(features, weight, preferred_element_type=jnp.float32).astype(jnp.bfloat16)
    blk_size = lax.axis_size("blk")
    chunks = 2
    chunk_width = feature_width // chunks
    activated_parts = []
    grad_parts = []
    bias_parts = []
    for chunk in range(chunks):
        columns = slice(chunk * chunk_width, (chunk + 1) * chunk_width)
        shard_rows = gather_by_exchange(projected[:, columns], "blk", blk_size).reshape(
            -1, chunk_width
        )
        partial_value = forward_spmm(row_lists, tile_stack, shard_rows, row_tiles)
        by_core = partial_value.reshape(row_tiles * tile_size, chunk_width)
        core_sum = reduce_by_exchange(by_core, "core", core_size).astype(jnp.bfloat16)
        preact = reduce_by_exchange(core_sum, "rh", chip_size) + bias_vector[columns]
        own_grad = (grad_out[:, columns].astype(jnp.float32) * silu_slope(preact)).astype(
            jnp.bfloat16
        )
        activated_parts.append(jax.nn.silu(preact).astype(jnp.bfloat16))
        chip_grad = gather_by_exchange(own_grad, "rh", chip_size).reshape(-1, chunk_width)
        pre_grad = gather_by_exchange(chip_grad, "core", core_size)
        grad_tiles = pre_grad.reshape(row_tiles, tile_size, chunk_width)
        column_contribution = backward_spmm(row_lists, tile_stack, grad_tiles)
        partition_bias = jnp.sum(grad_tiles.astype(jnp.float32), axis=(0, 1))
        bias_high = partition_bias.astype(jnp.bfloat16)
        bias_low = (partition_bias - bias_high.astype(jnp.float32)).astype(jnp.bfloat16)
        extra = jnp.zeros((16, chunk_width), jnp.bfloat16).at[0].set(bias_high).at[1].set(bias_low)
        pieces = jnp.concatenate(
            [
                column_contribution.reshape(blk_size, dev_rows, chunk_width),
                jnp.broadcast_to(extra[None], (blk_size, 16, chunk_width)),
            ],
            axis=1,
        )
        received = lax.all_to_all(pieces, "blk", 0, 0, tiled=True)
        summed = jnp.sum(received.astype(jnp.float32), axis=0)
        grad_parts.append(summed[:dev_rows].astype(jnp.bfloat16))
        bias_parts.append(summed[dev_rows] + summed[dev_rows + 1])
    activated = jnp.concatenate(activated_parts, axis=1)
    proj_grad = jnp.concatenate(grad_parts, axis=1)
    bias_sum = jnp.concatenate(bias_parts, axis=0)
    local_weight = jnp.einsum("nf,ng->fg", features, proj_grad, preferred_element_type=jnp.float32)
    device_count = blk_size * rep_size
    every = ("blk", "rh", "core")
    reduced = reduce_by_exchange(local_weight, every, device_count)
    weight_sum = (
        gather_by_exchange(reduced.astype(jnp.bfloat16), every, device_count)
        .reshape(-1, feature_width)
        .astype(jnp.float32)
    )
    feature_grad = jnp.einsum(
        "ng,fg->nf", proj_grad, weight, preferred_element_type=jnp.float32
    ).astype(jnp.bfloat16)
    return (projected, activated, feature_grad, weight_sum / root_count, bias_sum / root_count)


def solution(mesh):
    blk_count, rep_count = mesh.devices.shape
    chip_mesh = Mesh(mesh.devices.reshape(blk_count, rep_count // 2, 2), ("blk", "rh", "core"))
    return jax.shard_map(
        per_device,
        mesh=chip_mesh,
        in_specs=(
            P(("blk", "rh", "core"), None),
            P("blk", None, None),
            P(),
            P(),
            P("blk", ("rh", "core"), None, None),
            P("blk", ("rh", "core"), None, None, None, None),
            P(("blk", "rh", "core"), None),
        ),
        out_specs=(
            P(("blk", "rh", "core"), None),
            P(("blk", "rh", "core"), None),
            P(("blk", "rh", "core"), None),
            P(),
            P(),
        ),
        check_vma=False,
    )
```

```python
import functools
import math

import jax
import jax.numpy as jnp
from jax import lax
from jax.experimental import pallas as pl
from jax.experimental.pallas import tpu as pltpu
from jax.sharding import Mesh
from jax.sharding import PartitionSpec as P


def silu_slope(values):
    sigma = jax.nn.sigmoid(values)
    return sigma * (1.0 + values * (1.0 - sigma))


def _forward_kernel(rows_ref, first_ref, touched_ref, tiles_ref, cols_ref, out_ref, acc_ref):
    step = pl.program_id(0)
    fill = tiles_ref.shape[1]
    inputs = cols_ref[...]
    for j in range(fill):
        target = rows_ref[step, j]
        product = jnp.dot(tiles_ref[0, j], inputs, preferred_element_type=jnp.float32)
        acc_ref[target] = jnp.where(first_ref[step, j] == 1, product, acc_ref[target] + product)

    @pl.when(step == pl.num_programs(0) - 1)
    def _():
        for tile in range(acc_ref.shape[0]):
            out_ref[tile] = jnp.where(touched_ref[tile] == 1, acc_ref[tile], 0.0).astype(
                out_ref.dtype
            )


def forward_spmm(row_lists, tile_stack, shard_rows, row_tiles, interpret=False):
    col_tiles, fill, tile_size, _ = tile_stack.shape
    width = shard_rows.shape[1]
    flat = row_lists.reshape(-1)
    order = jnp.arange(flat.shape[0], dtype=jnp.int32)
    same = flat[:, None] == flat[None, :]
    earlier = order[None, :] < order[:, None]
    first_flags = (~jnp.any(same & earlier, axis=1)).astype(jnp.int32).reshape(row_lists.shape)
    tiles = jnp.arange(row_tiles, dtype=jnp.int32)
    touched = jnp.any(flat[None, :] == tiles[:, None], axis=1).astype(jnp.int32)
    grid_spec = pltpu.PrefetchScalarGridSpec(
        num_scalar_prefetch=3,
        grid=(col_tiles,),
        in_specs=[
            pl.BlockSpec((1, fill, tile_size, tile_size), lambda c, rows, first, hit: (c, 0, 0, 0)),
            pl.BlockSpec((tile_size, width), lambda c, rows, first, hit: (c, 0)),
        ],
        out_specs=pl.BlockSpec(
            (row_tiles, tile_size, width), lambda c, rows, first, hit: (0, 0, 0)
        ),
        scratch_shapes=[pltpu.VMEM((row_tiles, tile_size, width), jnp.float32)],
    )
    return pl.pallas_call(
        _forward_kernel,
        grid_spec=grid_spec,
        out_shape=jax.ShapeDtypeStruct((row_tiles, tile_size, width), jnp.bfloat16),
        compiler_params=pltpu.CompilerParams(
            dimension_semantics=("arbitrary",), vmem_limit_bytes=56 * 1024 * 1024
        ),
        interpret=interpret,
    )(row_lists, first_flags, touched, tile_stack, shard_rows)


def _backward_kernel(rows_ref, tiles_ref, grad_ref, out_ref):
    step = pl.program_id(0)
    fill = tiles_ref.shape[1]
    total = None
    for j in range(fill):
        source = rows_ref[step, j]
        part = lax.dot_general(
            tiles_ref[0, j],
            grad_ref[source],
            (((0,), (0,)), ((), ())),
            preferred_element_type=jnp.float32,
        )
        total = part if total is None else total + part
    out_ref[...] = total.astype(out_ref.dtype)


def backward_spmm(row_lists, tile_stack, grad_tiles, interpret=False):
    col_tiles, fill, tile_size, _ = tile_stack.shape
    row_tiles, _, width = grad_tiles.shape
    grid_spec = pltpu.PrefetchScalarGridSpec(
        num_scalar_prefetch=1,
        grid=(col_tiles,),
        in_specs=[
            pl.BlockSpec((1, fill, tile_size, tile_size), lambda c, rows: (c, 0, 0, 0)),
            pl.BlockSpec((row_tiles, tile_size, width), lambda c, rows: (0, 0, 0)),
        ],
        out_specs=pl.BlockSpec((tile_size, width), lambda c, rows: (c, 0)),
    )
    return pl.pallas_call(
        _backward_kernel,
        grid_spec=grid_spec,
        out_shape=jax.ShapeDtypeStruct((col_tiles * tile_size, width), jnp.bfloat16),
        compiler_params=pltpu.CompilerParams(
            dimension_semantics=("arbitrary",), vmem_limit_bytes=56 * 1024 * 1024
        ),
        interpret=interpret,
    )(row_lists, tile_stack, grad_tiles)


def gather_by_exchange(values, axis, count):
    stacked = jnp.broadcast_to(values[None], (count,) + values.shape)
    return lax.all_to_all(stacked, axis, 0, 0, tiled=True)


def reduce_by_exchange(values, axis, count):
    chunks = values.reshape((count, values.shape[0] // count) + values.shape[1:])
    received = lax.all_to_all(chunks, axis, 0, 0, tiled=True)
    return jnp.sum(received.astype(jnp.float32), axis=0)


def per_device(raw_features, move_plan, weight, bias_vector, tile_rows, tile_values, grad_out):
    core_size = lax.axis_size("core")
    chip_size = lax.axis_size("rh")
    rep_size = chip_size * core_size
    own_index = lax.axis_index("rh") * core_size + lax.axis_index("core")
    dev_rows, feature_width = grad_out.shape
    raw_rows = raw_features.shape[0]
    capacity = 4 * (dev_rows // (2 * rep_size))
    counts = move_plan[0]
    tile_stack = tile_values[0, 0]
    tile_lists = tile_rows[0, 0]
    tile_size = tile_stack.shape[2]
    row_tiles = rep_size * dev_rows // tile_size
    root_count = math.sqrt(dev_rows * lax.axis_size("blk") * rep_size)
    sent_counts = lax.dynamic_index_in_dim(counts, own_index, 0, keepdims=False)
    first_rows = jnp.cumsum(sent_counts) - sent_counts
    slot_rows = first_rows[:, None] + jnp.arange(capacity, dtype=jnp.int32)[None, :]
    outgoing = raw_features[jnp.minimum(slot_rows, raw_rows - 1)]
    incoming = lax.all_to_all(outgoing, ("rh", "core"), split_axis=0, concat_axis=0, tiled=True)
    block_tiles = dev_rows // tile_size
    block_of = tile_lists // block_tiles
    row_lists = (
        (block_of % core_size) * (chip_size * block_tiles)
        + (block_of // core_size) * block_tiles
        + tile_lists % block_tiles
    )
    recv_counts = lax.dynamic_index_in_dim(counts, own_index, 1, keepdims=False)
    inclusive = jnp.cumsum(recv_counts)
    exclusive = inclusive - recv_counts
    positions = jnp.arange(dev_rows, dtype=jnp.int32)
    sources = jnp.sum((inclusive[None, :] <= positions[:, None]).astype(jnp.int32), axis=1)
    selector = sources[:, None] == jnp.arange(rep_size, dtype=jnp.int32)[None, :]
    offsets = jnp.sum(jnp.where(selector, exclusive[None, :], 0), axis=1)
    features = incoming.reshape(rep_size * capacity, feature_width)[
        sources * capacity + positions - offsets
    ]
    projected = jnp.dot(features, weight, preferred_element_type=jnp.float32).astype(jnp.bfloat16)
    blk_size = lax.axis_size("blk")
    chunks = 2
    chunk_width = feature_width // chunks
    activated_parts = []
    grad_parts = []
    bias_parts = []
    for chunk in range(chunks):
        columns = slice(chunk * chunk_width, (chunk + 1) * chunk_width)
        shard_rows = gather_by_exchange(projected[:, columns], "blk", blk_size).reshape(
            -1, chunk_width
        )
        partial_value = forward_spmm(row_lists, tile_stack, shard_rows, row_tiles)
        by_core = partial_value.reshape(row_tiles * tile_size, chunk_width)
        core_sum = reduce_by_exchange(by_core, "core", core_size).astype(jnp.bfloat16)
        preact = reduce_by_exchange(core_sum, "rh", chip_size) + bias_vector[columns]
        own_grad = (grad_out[:, columns].astype(jnp.float32) * silu_slope(preact)).astype(
            jnp.bfloat16
        )
        activated_parts.append(jax.nn.silu(preact).astype(jnp.bfloat16))
        chip_grad = gather_by_exchange(own_grad, "rh", chip_size).reshape(-1, chunk_width)
        pre_grad = gather_by_exchange(chip_grad, "core", core_size)
        grad_tiles = pre_grad.reshape(row_tiles, tile_size, chunk_width)
        column_contribution = backward_spmm(row_lists, tile_stack, grad_tiles)
        partition_bias = jnp.sum(grad_tiles.astype(jnp.float32), axis=(0, 1))
        bias_high = partition_bias.astype(jnp.bfloat16)
        bias_low = (partition_bias - bias_high.astype(jnp.float32)).astype(jnp.bfloat16)
        extra = jnp.zeros((16, chunk_width), jnp.bfloat16).at[0].set(bias_high).at[1].set(bias_low)
        pieces = jnp.concatenate(
            [
                column_contribution.reshape(blk_size, dev_rows, chunk_width),
                jnp.broadcast_to(extra[None], (blk_size, 16, chunk_width)),
            ],
            axis=1,
        )
        received = lax.all_to_all(pieces, "blk", 0, 0, tiled=True)
        summed = jnp.sum(received.astype(jnp.float32), axis=0)
        grad_parts.append(summed[:dev_rows].astype(jnp.bfloat16))
        bias_parts.append(summed[dev_rows] + summed[dev_rows + 1])
    activated = jnp.concatenate(activated_parts, axis=1)
    proj_grad = jnp.concatenate(grad_parts, axis=1)
    bias_sum = jnp.concatenate(bias_parts, axis=0)
    local_weight = jnp.einsum("nf,ng->fg", features, proj_grad, preferred_element_type=jnp.float32)
    device_count = blk_size * rep_size
    every = ("blk", "rh", "core")
    reduced = reduce_by_exchange(local_weight.reshape(-1, 128), every, device_count)
    weight_sum = (
        gather_by_exchange(reduced.astype(jnp.bfloat16), every, device_count)
        .reshape(-1, feature_width)
        .astype(jnp.float32)
    )
    feature_grad = jnp.einsum(
        "ng,fg->nf", proj_grad, weight, preferred_element_type=jnp.float32
    ).astype(jnp.bfloat16)
    return (projected, activated, feature_grad, weight_sum / root_count, bias_sum / root_count)


def solution(mesh):
    blk_count, rep_count = mesh.devices.shape
    chip_mesh = Mesh(mesh.devices.reshape(blk_count, rep_count // 2, 2), ("blk", "rh", "core"))
    return jax.shard_map(
        per_device,
        mesh=chip_mesh,
        in_specs=(
            P(("blk", "rh", "core"), None),
            P("blk", None, None),
            P(),
            P(),
            P("blk", ("rh", "core"), None, None),
            P("blk", ("rh", "core"), None, None, None, None),
            P(("blk", "rh", "core"), None),
        ),
        out_specs=(
            P(("blk", "rh", "core"), None),
            P(("blk", "rh", "core"), None),
            P(("blk", "rh", "core"), None),
            P(),
            P(),
        ),
        check_vma=False,
    )
```
